32 devices in a mesh: tile: 8 (over z, x), chan: 4 (over y, core).
Axes of the slice: x: 2, y: 2, z: 4, core: 2. Of those that a mesh axis runs over, the one named last changes fastest.
Arguments:
- visibilities: float32 [4, 2048, 128], P('chan', 'tile'), may hold values from -6 to 6
- kernels: bfloat16 [4, 32, 2, 64, 128], P('chan'), may hold values from -0.75 to 0.75
- destination: int32 [4, 2048, 1], P('chan', 'tile'), may hold values from 0 to 7; in each aligned block of 256 rows (0 to 255, 256 to 511, ..., all dimensions but the last counted through in order) at most 96 rows name the same one
- cell: int32 [4, 2048], P('chan', 'tile'), may hold values from 0 to 2047
- plane: int32 [4, 2048], P('chan', 'tile'), may hold values from 0 to 31
Outputs:
- image: float32 [1024, 1024], P('chan', 'tile')
The draws below stay inside these ranges and needn't reach their ends.
Inputs may be any that keep to these rules, and one draw needn't show every extreme that they name: `destination`: in the rows of one device (aligned blocks of 256 rows), no tile is named more than 96 times; some tile is named exactly 96 times in some devices' rows.
All inputs are finite; a program needn't handle non-finite values.
Results may differ from the reference program's by a relative error of at most 0.0059.
Values may be sent and summed in bfloat16 or wider, within the bound.
No kernel may reach another device: no remote copies, remote signals or barrier semaphores. Data moves between devices by JAX's collectives and lax.ppermute only.
A program may use at most 384 MiB of HBM per device.

```python
import math
import jax
import jax.numpy as jnp
import numpy as np
from jax import lax

G = 8192
S = 64
K = 64
NW = 32
P_SIZE = 1024
BLK_DEV = 256
CAP = 96
NCG = 4
BASE = 2048
CELLS_T = 2048
N_TILE = 8


def place_ends(drawn, key, least, largest):
    place = [jax.random.randint(jax.random.fold_in(key, axis), (), 0, length) for axis, length in enumerate(drawn.shape)]
    main_axis = drawn.shape.index(max(drawn.shape))
    beside = place[:main_axis] + [(place[main_axis] + 1) % drawn.shape[main_axis]] + place[main_axis + 1:]
    return drawn.at[tuple(place)].set(least).at[tuple(beside)].set(largest)


def shard_levels(own_key, shape, cuts, least, high):
    def one(axis_at, shards_of):
        heights = jax.random.uniform(jax.random.fold_in(jax.random.fold_in(own_key, 6), axis_at), (shards_of,), jnp.float32, least / len(cuts), high / len(cuts))
        return jnp.repeat(jnp.exp(heights), shape[axis_at] // shards_of).reshape((-1,) + (1,) * (len(shape) - axis_at - 1))

    factor_of = one(*cuts[0])
    for cut in cuts[1:]:
        factor_of = factor_of * one(*cut)
    return factor_of


def assign_block(own_key, own, number, rows, number_of, top, limit, skew):
    order = jax.random.permutation(own_key, number_of)
    heavy_load, common = shares(number_of, rows * top, limit, skew, True), shares(number_of, rows * top, limit, skew, False)
    places = jnp.arange(number_of)

    def named(sizes, rotation):
        used = int((sizes > 0).sum())
        fixed = max(1, used // 4)
        shifted = fixed + (places - fixed + rotation * (used - fixed)) % max(1, number_of - fixed)
        return jnp.zeros((number_of,), jnp.int32).at[order[jnp.where(places < fixed, places, shifted)]].set(jnp.asarray(sizes, jnp.int32))

    sizes = jnp.where(number % 4 == 0, named(heavy_load, number // 4), named(common, number - number // 4 - 1))
    mixed = jax.random.permutation(jax.random.fold_in(own, 3), number_of)
    giver, taker = mixed[0:number_of // 2 * 2:2], mixed[1:number_of // 2 * 2:2]
    margin = jnp.minimum(sizes[giver] - 1, limit - sizes[taker]) // 2
    margin = jnp.where((giver == order[0]) | (taker == order[0]) | (sizes[taker] == 0), 0, jnp.maximum(margin, 0))
    shifted = jax.random.randint(jax.random.fold_in(own, 4), (number_of // 2,), 0, 1 << 20) % (margin + 1)
    sizes = sizes.at[giver].add(-shifted).at[taker].add(shifted)
    items = jnp.searchsorted(jnp.cumsum(sizes), jnp.arange(rows * top), side="right").astype(jnp.int32)
    grid = items.reshape(top, rows).T
    grid = grid[jax.random.permutation(jax.random.fold_in(own, 1), rows)]
    rotation = jax.random.randint(jax.random.fold_in(own, 2), (rows, 1), 0, top)
    return jnp.take_along_axis(grid, (jnp.arange(top)[None, :] + rotation) % top, axis=1)


def shares(number_of, total, reach, slope, full):
    portions = [(1 << 20) // math.isqrt(standing ** slope) + 1 for standing in range(1, number_of + 1)]
    largest = reach if full else min(reach, max(-(-total // number_of), total * portions[0] // sum(portions)))
    least = 1 if total - largest >= number_of - 1 else 0
    counts, rest = [largest] + [least] * (number_of - 1), total - largest - least * (number_of - 1)
    while rest > 0:
        movable = [i for i in range(1, number_of) if counts[i] < largest] or [i for i in range(1, number_of) if counts[i] < reach]
        mass, remaining = sum([portions[i] for i in movable]), rest
        for i in movable:
            addition = min(reach - counts[i], max(1, remaining * portions[i] // mass), rest)
            counts[i] = counts[i] + addition
            rest = rest - addition
    return np.array(counts)


def bell_draw(stream_key, dims, width, reach, cuts=(), kind=jnp.bfloat16):
    loudness = shard_levels(stream_key, dims, cuts, -0.22, 0.18) if cuts else 1.0
    array = jax.random.normal(stream_key, dims, jnp.float32) * width * loudness
    return jnp.minimum(jnp.maximum(array, -reach), reach).astype(kind)


def setup_inputs(seed: int = 0) -> dict:
    splits = jax.random.split(jax.random.key(seed), 6)
    visibilities = bell_draw(splits[0], (NCG, BASE, 2 * K), 1.0, 6.0, ((0, 4), (1, 8)), jnp.float32)
    kernels = bell_draw(splits[1], (NCG, NW, 2, K, 2 * S), K ** -0.5, 0.75, ((0, 4),))
    destination_keys = jax.random.split(jax.random.fold_in(splits[2], 1), NCG * BASE // BLK_DEV)
    destination_turns = jax.random.permutation(jax.random.fold_in(splits[2], 3), NCG * BASE // BLK_DEV)
    destination = jax.vmap(lambda own, number: assign_block(jax.random.fold_in(splits[2], 2), own, number, BLK_DEV, N_TILE, 1, CAP, 2))(destination_keys, destination_turns).reshape((NCG, BASE, 1))
    cell = place_ends(jax.random.randint(splits[3], (NCG, BASE), 0, CELLS_T), jax.random.fold_in(splits[3], 1), 0, CELLS_T - 1).astype(jnp.int32)
    plane = place_ends(jax.random.randint(splits[4], (NCG, BASE), 0, NW), jax.random.fold_in(splits[4], 1), 0, NW - 1).astype(jnp.int32)
    return {"visibilities": visibilities, "kernels": kernels, "destination": destination, "cell": cell, "plane": plane}


def round_half(values):
    return lax.optimization_barrier(values.astype(jnp.bfloat16)).astype(jnp.float32)


def phase_tables(first_row, row_count, grid_width, pixels):
    spacing = grid_width // pixels - 1
    row_index = first_row + jnp.arange(row_count, dtype=jnp.int32)
    pixel_index = jnp.arange(pixels, dtype=jnp.int32)
    product = jnp.mod((row_index[:, None] - grid_width // 2) * (spacing * (pixel_index[None, :] - pixels // 2)), grid_width)
    phase_angle = product.astype(jnp.float32) * (2.0 * math.pi / grid_width)
    return round_half(jnp.cos(phase_angle)), round_half(jnp.sin(phase_angle))


def block_patches(samples, kernel_rows):
    sample_count = samples.shape[1] // 2
    support = kernel_rows.shape[3] // 2
    vis_real = samples[:, :sample_count, None]
    vis_imag = samples[:, sample_count:, None]
    kern_real = kernel_rows[:, 0, :, support:].astype(jnp.float32)
    kern_imag = kernel_rows[:, 1, :, support:].astype(jnp.float32)
    weighted_real = round_half(vis_real * kern_real - vis_imag * kern_imag)
    weighted_imag = round_half(vis_real * kern_imag + vis_imag * kern_real)
    u_kernel = kernel_rows[:, :, :, :support].astype(jnp.float32)
    v_weighted = jnp.stack([jnp.stack([weighted_real, weighted_imag], 2), jnp.stack([-weighted_imag, weighted_real], 2)], 1)
    return jnp.einsum('bpkx,bpkqy->bxqy', u_kernel, v_weighted)


def reference(visibilities, kernels, destination, cell, plane):
    groups = visibilities.shape[0]
    slab_rows = G // N_TILE
    cell_cols = G // S
    slot_total = N_TILE * CAP
    stride = math.gcd(slot_total, 256)
    cosine, sine = phase_tables(0, G, G, P_SIZE)
    cosine_cells = cosine.reshape(cell_cols, S, P_SIZE)
    sine_cells = sine.reshape(cell_cols, S, P_SIZE)

    def one_slab(image_acc, packed):
        group_id, tile_id = packed
        samples_all = lax.dynamic_index_in_dim(visibilities, group_id, 0, keepdims=False)
        kernel_set = lax.dynamic_index_in_dim(kernels, group_id, 0, keepdims=False)
        owners = lax.dynamic_index_in_dim(destination, group_id, 0, keepdims=False)[:, 0]
        cell_ids = lax.dynamic_index_in_dim(cell, group_id, 0, keepdims=False)
        plane_ids = lax.dynamic_index_in_dim(plane, group_id, 0, keepdims=False)
        sorted_ids = jnp.argsort(owners, stable=True).astype(jnp.int32)
        amount = jnp.sum((owners == tile_id).astype(jnp.int32))
        first = jnp.sum((owners < tile_id).astype(jnp.int32))
        padded_ids = jnp.concatenate([sorted_ids, jnp.zeros((slot_total,), jnp.int32)])
        chosen = lax.dynamic_slice_in_dim(padded_ids, first, slot_total)
        in_use = (jnp.arange(slot_total, dtype=jnp.int32) < amount).astype(samples_all.dtype)
        samples = samples_all[chosen] * in_use[:, None]
        samples = samples.reshape(slot_total // stride, stride, samples.shape[1])
        cell_slot = cell_ids[chosen].reshape(slot_total // stride, stride)
        plane_slot = plane_ids[chosen].reshape(slot_total // stride, stride)

        def add_block(grid_cells, blk):
            sample_blk, cell_blk, plane_blk = blk
            patches = block_patches(sample_blk, kernel_set[plane_blk])
            return grid_cells.at[cell_blk].add(patches), None

        grid_start = jnp.zeros((CELLS_T, S, 2, S), jnp.float32)
        grid_cells, _ = lax.scan(add_block, grid_start, (samples, cell_slot, plane_slot))
        grid_round = round_half(grid_cells).reshape(slab_rows // S, cell_cols, S, 2, S)
        with_cosine = jnp.einsum('acxpy,cym->pmax', grid_round, cosine_cells).reshape(2, P_SIZE, slab_rows)
        with_sine = jnp.einsum('acxpy,cym->pmax', grid_round, sine_cells).reshape(2, P_SIZE, slab_rows)
        transformed_real = round_half(with_cosine[0] - with_sine[1])
        transformed_imag = round_half(with_sine[0] + with_cosine[1])
        own_cosine = lax.dynamic_slice_in_dim(cosine, tile_id * slab_rows, slab_rows, 0)
        own_sine = lax.dynamic_slice_in_dim(sine, tile_id * slab_rows, slab_rows, 0)
        partial_image = jnp.dot(transformed_real, own_cosine, preferred_element_type=jnp.float32) - jnp.dot(transformed_imag, own_sine, preferred_element_type=jnp.float32)
        return image_acc + partial_image, None

    group_ids = jnp.repeat(jnp.arange(groups, dtype=jnp.int32), N_TILE)
    tile_ids = jnp.tile(jnp.arange(N_TILE, dtype=jnp.int32), groups)
    image_acc, _ = lax.scan(one_slab, jnp.zeros((P_SIZE, P_SIZE), jnp.float32), (group_ids, tile_ids))
    return image_acc.T * (1.0 / G)
```

```python
import math

import jax
import jax.numpy as jnp
from jax import lax
from jax.sharding import PartitionSpec as P

G = 8192
S = 64
NW = 32
P_SIZE = 1024
NF = 8


def block_patches(samples, kernel_rows):
    sample_count = samples.shape[1] // 2
    support = kernel_rows.shape[3] // 2
    vis_real = samples[:, :sample_count, None]
    vis_imag = samples[:, sample_count:, None]
    kern_real = kernel_rows[:, 0, :, support:].astype(jnp.float32)
    kern_imag = kernel_rows[:, 1, :, support:].astype(jnp.float32)
    weighted_real = (vis_real * kern_real - vis_imag * kern_imag).astype(jnp.bfloat16)
    weighted_imag = (vis_real * kern_imag + vis_imag * kern_real).astype(jnp.bfloat16)
    u_kernel = kernel_rows[:, :, :, :support]
    v_weighted = jnp.stack(
        [
            jnp.stack([weighted_real, weighted_imag], 2),
            jnp.stack([-weighted_imag, weighted_real], 2),
        ],
        1,
    )
    return jnp.einsum("bpkx,bpkqy->bxqy", u_kernel, v_weighted, preferred_element_type=jnp.float32)


def phase_index(rows, cols):
    spacing = G // P_SIZE - 1
    return jnp.mod(rows[:, None] * (spacing * cols[None, :]), G)


def cos_sin(index):
    angle = index.astype(jnp.float32) * (2.0 * math.pi / G)
    return jnp.cos(angle).astype(jnp.bfloat16), jnp.sin(angle).astype(jnp.bfloat16)


def local(visibilities, kernels, destination, cell, plane):
    tile_count = lax.axis_size("tile")
    tile_index = lax.axis_index("tile")
    samples = visibilities[0]
    kernel_set = kernels[0]
    owners = destination[0, :, 0]
    blocks = samples.shape[0]
    capacity = 3 * blocks // tile_count
    spacing = G // P_SIZE - 1

    counts = jnp.sum(
        (owners[:, None] == jnp.arange(tile_count, dtype=jnp.int32)[None, :]).astype(jnp.int32), axis=0
    )
    first = jnp.cumsum(counts) - counts
    order = jnp.argsort(owners, stable=True).astype(jnp.int32)
    slot = jnp.arange(capacity, dtype=jnp.int32)
    valid = slot[None, :] < counts[:, None]
    src = order[jnp.clip(first[:, None] + slot[None, :], 0, blocks - 1)]
    packed_meta = cell[0] * NW + plane[0]
    send_samples = jnp.where(valid[:, :, None], samples[src], 0.0)
    send_meta = jnp.where(valid, packed_meta[src], 0)
    arrived = lax.all_to_all(send_samples, "tile", split_axis=0, concat_axis=0, tiled=True)
    arrived_meta = lax.all_to_all(send_meta, "tile", split_axis=0, concat_axis=0, tiled=True)
    slot_total = tile_count * capacity
    arrived = arrived.reshape(slot_total, samples.shape[1])
    arrived_meta = arrived_meta.reshape(slot_total)

    slab_rows = G // tile_count
    row_cells = slab_rows // S
    cell_cols = G // S
    q_len = G // NF
    q_cells = q_len // S
    j_len = P_SIZE // NF

    cell_r = arrived_meta // NW
    plane_r = arrived_meta % NW
    patches = block_patches(arrived, kernel_set[plane_r])
    rotated = jnp.stack([-patches[:, :, 1, :], patches[:, :, 0, :]], axis=2)
    p2 = jnp.stack([patches, rotated], axis=1).astype(jnp.bfloat16).reshape(slot_total, 2, S * 2 * S)

    a_s = cell_r // cell_cols
    cc_s = cell_r % cell_cols
    p_s = cc_s // q_cells
    qc_s = cc_s % q_cells
    resid = jnp.arange(NF, dtype=jnp.int32)
    ph_index = jnp.mod(spacing * (p_s[:, None] - NF // 2) * resid[None, :], NF)
    ph_angle = ph_index.astype(jnp.float32) * (2.0 * math.pi / NF)
    phase = jnp.stack([jnp.cos(ph_angle), jnp.sin(ph_angle)], axis=-1)
    place = (a_s[:, None] == jnp.arange(row_cells, dtype=jnp.int32)[None, :])[:, :, None] & (
        qc_s[:, None] == jnp.arange(q_cells, dtype=jnp.int32)[None, :]
    )[:, None, :]
    l2 = (place.astype(jnp.float32)[None, :, :, :, None] * jnp.transpose(phase, (1, 0, 2))[:, :, None, None, :])
    l2 = jnp.transpose(l2, (0, 2, 3, 1, 4)).astype(jnp.bfloat16)
    folded = jnp.einsum("raqsk,skn->raqn", l2, p2, preferred_element_type=jnp.float32).astype(jnp.bfloat16)
    folded = folded.reshape(NF, row_cells, q_cells, S, 2 * S)

    q_index = jnp.arange(q_len, dtype=jnp.int32)
    j_index = resid[:, None] + NF * (jnp.arange(j_len, dtype=jnp.int32)[None, :] - j_len // 2)
    idx1 = jnp.mod(q_index[None, :, None] * (spacing * j_index[:, None, :]), G)
    c1, s1 = cos_sin(idx1)
    w1 = jnp.stack([jnp.stack([c1, s1], axis=2), jnp.stack([-s1, c1], axis=2)], axis=2)
    w1 = w1.reshape(NF, q_cells, S, 2, 2, j_len)
    w1 = jnp.transpose(w1, (0, 1, 3, 2, 4, 5)).reshape(NF, q_cells, 2 * S, 2 * j_len)
    transformed = jnp.einsum("raqxk,rqkn->raxn", folded, w1, preferred_element_type=jnp.float32)
    transformed = transformed.astype(jnp.bfloat16).reshape(NF, slab_rows, 2, j_len)

    u_index = tile_index * slab_rows + jnp.arange(slab_rows, dtype=jnp.int32) - G // 2
    l_index = jnp.arange(P_SIZE, dtype=jnp.int32) - P_SIZE // 2
    c2, s2 = cos_sin(phase_index(u_index, l_index))
    e2 = jnp.stack([c2, -s2])
    partial = jnp.einsum("iul,ruij->lrj", e2, transformed, preferred_element_type=jnp.float32)
    partial = lax.psum_scatter(partial, "chan", scatter_dimension=0, tiled=True)
    partial = lax.psum_scatter(partial, "tile", scatter_dimension=2, tiled=True)
    out = jnp.transpose(partial, (0, 2, 1))
    return out.reshape(out.shape[0], -1) * (1.0 / G)


def solution(mesh):
    placed = (
        P("chan", "tile", None),
        P("chan", None, None, None, None),
        P("chan", "tile", None),
        P("chan", "tile"),
        P("chan", "tile"),
    )
    return jax.shard_map(
        local, mesh=mesh, in_specs=placed, out_specs=P("chan", "tile"), check_vma=False
    )
```

```python
import math

import jax
import jax.numpy as jnp
from jax import lax
from jax.sharding import PartitionSpec as P

G = 8192
S = 64
NW = 32
P_SIZE = 1024
NF = 8


def block_patches(samples, kernel_rows):
    sample_count = samples.shape[1] // 2
    support = kernel_rows.shape[3] // 2
    vis_real = samples[:, :sample_count, None]
    vis_imag = samples[:, sample_count:, None]
    kern_real = kernel_rows[:, 0].astype(jnp.float32)
    kern_imag = kernel_rows[:, 1].astype(jnp.float32)
    full_real = (vis_real * kern_real - vis_imag * kern_imag).astype(jnp.bfloat16)
    full_imag = (vis_real * kern_imag + vis_imag * kern_real).astype(jnp.bfloat16)
    weighted_real = full_real[:, :, support:]
    weighted_imag = full_imag[:, :, support:]
    v_weighted = jnp.stack(
        [
            jnp.concatenate([weighted_real, weighted_imag], axis=-1),
            jnp.concatenate([-weighted_imag, weighted_real], axis=-1),
        ],
        1,
    )
    patch = jnp.einsum("bpkx,bpkn->bxn", kernel_rows, v_weighted, preferred_element_type=jnp.float32)
    return patch[:, :support, :]


def phase_index(rows, cols):
    spacing = G // P_SIZE - 1
    return jnp.mod(rows[:, None] * (spacing * cols[None, :]), G)


def cos_sin_f32(index):
    angle = index.astype(jnp.float32) * (2.0 * math.pi / G)
    return jnp.cos(angle), jnp.sin(angle)


def local(visibilities, kernels, destination, cell, plane):
    tile_count = lax.axis_size("tile")
    tile_index = lax.axis_index("tile")
    samples = visibilities[0]
    kernel_set = kernels[0]
    owners = destination[0, :, 0]
    blocks = samples.shape[0]
    capacity = 3 * blocks // tile_count
    spacing = G // P_SIZE - 1

    counts = jnp.sum(
        (owners[:, None] == jnp.arange(tile_count, dtype=jnp.int32)[None, :]).astype(jnp.int32), axis=0
    )
    first = jnp.cumsum(counts) - counts
    order = jnp.argsort(owners, stable=True).astype(jnp.int32)
    slot = jnp.arange(capacity, dtype=jnp.int32)
    valid = slot[None, :] < counts[:, None]
    src = order[jnp.clip(first[:, None] + slot[None, :], 0, blocks - 1)]
    packed_meta = cell[0] * NW + plane[0]
    send_samples = jnp.where(valid[:, :, None], samples[src], 0.0)
    send_meta = jnp.where(valid, packed_meta[src], 0)
    arrived = lax.all_to_all(send_samples, "tile", split_axis=0, concat_axis=0, tiled=True)
    arrived_meta = lax.all_to_all(send_meta, "tile", split_axis=0, concat_axis=0, tiled=True)
    slot_total = tile_count * capacity
    arrived = arrived.reshape(slot_total, samples.shape[1])
    arrived_meta = arrived_meta.reshape(slot_total)

    slab_rows = G // tile_count
    row_cells = slab_rows // S
    cell_cols = G // S
    q_len = G // NF
    q_cells = q_len // S
    j_len = P_SIZE // NF

    cell_r = arrived_meta // NW
    plane_r = arrived_meta % NW
    patches = block_patches(arrived, kernel_set[plane_r])
    rotated = jnp.concatenate([-patches[:, :, S:], patches[:, :, :S]], axis=-1)
    p2 = jnp.stack([patches, rotated], axis=1).astype(jnp.bfloat16).reshape(slot_total, 2, S * 2 * S)

    a_s = cell_r // cell_cols
    cc_s = cell_r % cell_cols
    p_s = cc_s // q_cells
    qc_s = cc_s % q_cells
    resid = jnp.arange(NF, dtype=jnp.int32)
    ph_index = jnp.mod(spacing * (p_s[:, None] - NF // 2) * resid[None, :], NF)
    ph_angle = ph_index.astype(jnp.float32) * (2.0 * math.pi / NF)
    phase = jnp.stack([jnp.cos(ph_angle), jnp.sin(ph_angle)], axis=-1)
    place = (a_s[:, None] == jnp.arange(row_cells, dtype=jnp.int32)[None, :])[:, :, None] & (
        qc_s[:, None] == jnp.arange(q_cells, dtype=jnp.int32)[None, :]
    )[:, None, :]
    l2 = (place.astype(jnp.float32)[None, :, :, :, None] * jnp.transpose(phase, (1, 0, 2))[:, :, None, None, :])
    l2 = jnp.transpose(l2, (0, 2, 3, 1, 4)).astype(jnp.bfloat16)
    folded = jnp.einsum("raqsk,skn->raqn", l2, p2, preferred_element_type=jnp.float32).astype(jnp.bfloat16)
    folded = folded.reshape(NF, row_cells, q_cells, S, 2 * S)

    j_index = resid[:, None] + NF * (jnp.arange(j_len, dtype=jnp.int32)[None, :] - j_len // 2)
    coarse = jnp.arange(q_cells, dtype=jnp.int32) * S
    fine = jnp.arange(S, dtype=jnp.int32)
    ca, sa = cos_sin_f32(jnp.mod(coarse[None, :, None] * (spacing * j_index[:, None, :]), G))
    cb, sb = cos_sin_f32(jnp.mod(fine[None, :, None] * (spacing * j_index[:, None, :]), G))
    c1 = (ca[:, :, None, :] * cb[:, None, :, :] - sa[:, :, None, :] * sb[:, None, :, :]).astype(jnp.bfloat16)
    s1 = (sa[:, :, None, :] * cb[:, None, :, :] + ca[:, :, None, :] * sb[:, None, :, :]).astype(jnp.bfloat16)
    c1 = c1.reshape(NF, q_len, j_len)
    s1 = s1.reshape(NF, q_len, j_len)
    w1 = jnp.stack([jnp.stack([c1, s1], axis=2), jnp.stack([-s1, c1], axis=2)], axis=2)
    w1 = w1.reshape(NF, q_cells, S, 2, 2, j_len)
    w1 = jnp.transpose(w1, (0, 1, 3, 2, 4, 5)).reshape(NF, q_cells, 2 * S, 2 * j_len)
    transformed = jnp.einsum("raqxk,rqkn->raxn", folded, w1, preferred_element_type=jnp.float32)
    transformed = transformed.astype(jnp.bfloat16).reshape(NF, slab_rows, 2, j_len)

    l_index = jnp.arange(P_SIZE, dtype=jnp.int32) - P_SIZE // 2
    row_base = (tile_index * slab_rows - G // 2) + jnp.arange(row_cells, dtype=jnp.int32) * S
    ca, sa = cos_sin_f32(phase_index(row_base, l_index))
    cb, sb = cos_sin_f32(phase_index(fine, l_index))
    c2 = (ca[:, None, :] * cb[None, :, :] - sa[:, None, :] * sb[None, :, :]).astype(jnp.bfloat16)
    s2 = (sa[:, None, :] * cb[None, :, :] + ca[:, None, :] * sb[None, :, :]).astype(jnp.bfloat16)
    c2 = c2.reshape(slab_rows, P_SIZE)
    s2 = s2.reshape(slab_rows, P_SIZE)
    e2 = jnp.stack([c2, -s2])
    partial = jnp.einsum("iul,ruij->lrj", e2, transformed, preferred_element_type=jnp.float32)
    chan_count = lax.axis_size("chan")
    partial = partial.reshape(chan_count, P_SIZE // chan_count, NF, j_len)
    partial = jnp.sum(lax.all_to_all(partial, "chan", split_axis=0, concat_axis=0, tiled=True), axis=0)
    partial = partial.reshape(P_SIZE // chan_count, NF, tile_count, j_len // tile_count)
    partial = jnp.transpose(partial, (2, 0, 1, 3))
    partial = jnp.sum(lax.all_to_all(partial, "tile", split_axis=0, concat_axis=0, tiled=True), axis=0)
    out = jnp.transpose(partial, (0, 2, 1))
    return out.reshape(out.shape[0], -1) * (1.0 / G)


def solution(mesh):
    placed = (
        P("chan", "tile", None),
        P("chan", None, None, None, None),
        P("chan", "tile", None),
        P("chan", "tile"),
        P("chan", "tile"),
    )
    return jax.shard_map(
        local, mesh=mesh, in_specs=placed, out_specs=P("chan", "tile"), check_vma=False
    )
```

```python
import math

import jax
import jax.numpy as jnp
from jax import lax
from jax.sharding import PartitionSpec as P

G = 8192
S = 64
NW = 32
P_SIZE = 1024
NF = 8


def block_patches(samples, kernel_rows):
    sample_count = samples.shape[1] // 2
    support = kernel_rows.shape[3] // 2
    vis_real = samples[:, :sample_count, None]
    vis_imag = samples[:, sample_count:, None]
    kern_real = kernel_rows[:, 0].astype(jnp.float32)
    kern_imag = kernel_rows[:, 1].astype(jnp.float32)
    full_real = (vis_real * kern_real - vis_imag * kern_imag).astype(jnp.bfloat16)
    full_imag = (vis_real * kern_imag + vis_imag * kern_real).astype(jnp.bfloat16)
    weighted_real = full_real[:, :, support:]
    weighted_imag = full_imag[:, :, support:]
    v_weighted = jnp.stack(
        [
            jnp.concatenate([weighted_real, weighted_imag], axis=-1),
            jnp.concatenate([-weighted_imag, weighted_real], axis=-1),
        ],
        1,
    )
    patch = jnp.einsum("bpkx,bpkn->bxn", kernel_rows, v_weighted, preferred_element_type=jnp.float32)
    return patch[:, :support, :]


def phase_index(rows, cols):
    spacing = G // P_SIZE - 1
    return jnp.mod(rows[:, None] * (spacing * cols[None, :]), G)


def cos_sin_f32(index):
    angle = index.astype(jnp.float32) * (2.0 * math.pi / G)
    return jnp.cos(angle), jnp.sin(angle)


def local(visibilities, kernels, destination, cell, plane):
    tile_count = lax.axis_size("tile")
    tile_index = lax.axis_index("tile")
    samples = visibilities[0]
    kernel_set = kernels[0]
    owners = destination[0, :, 0]
    blocks = samples.shape[0]
    capacity = 3 * blocks // tile_count
    spacing = G // P_SIZE - 1

    counts = jnp.sum(
        (owners[:, None] == jnp.arange(tile_count, dtype=jnp.int32)[None, :]).astype(jnp.int32), axis=0
    )
    first = jnp.cumsum(counts) - counts
    order = jnp.argsort(owners, stable=True).astype(jnp.int32)
    slot = jnp.arange(capacity, dtype=jnp.int32)
    valid = slot[None, :] < counts[:, None]
    src = order[jnp.clip(first[:, None] + slot[None, :], 0, blocks - 1)]
    packed_meta = cell[0] * NW + plane[0]
    send_samples = jnp.where(valid[:, :, None], samples[src], 0.0)
    send_meta = jnp.where(valid, packed_meta[src], 0)
    arrived = lax.all_to_all(send_samples, "tile", split_axis=0, concat_axis=0, tiled=True)
    arrived_meta = lax.all_to_all(send_meta, "tile", split_axis=0, concat_axis=0, tiled=True)
    slot_total = tile_count * capacity
    arrived = arrived.reshape(slot_total, samples.shape[1])
    arrived_meta = arrived_meta.reshape(slot_total)

    slab_rows = G // tile_count
    row_cells = slab_rows // S
    cell_cols = G // S
    q_len = G // NF
    q_cells = q_len // S
    j_len = P_SIZE // NF

    cell_r = arrived_meta // NW
    plane_r = arrived_meta % NW
    patches = block_patches(arrived, kernel_set[plane_r])
    rotated = jnp.concatenate([-patches[:, :, S:], patches[:, :, :S]], axis=-1)
    p2 = jnp.stack([patches, rotated], axis=1).astype(jnp.bfloat16).reshape(slot_total, 2, S * 2 * S)

    a_s = cell_r // cell_cols
    cc_s = cell_r % cell_cols
    p_s = cc_s // q_cells
    qc_s = cc_s % q_cells
    resid = jnp.arange(NF, dtype=jnp.int32)
    ph_index = jnp.mod(spacing * (p_s[:, None] - NF // 2) * resid[None, :], NF)
    ph_angle = ph_index.astype(jnp.float32) * (2.0 * math.pi / NF)
    phase = jnp.stack([jnp.cos(ph_angle), jnp.sin(ph_angle)], axis=-1)
    place = (a_s[:, None] == jnp.arange(row_cells, dtype=jnp.int32)[None, :])[:, :, None] & (
        qc_s[:, None] == jnp.arange(q_cells, dtype=jnp.int32)[None, :]
    )[:, None, :]
    l2 = (place.astype(jnp.float32)[None, :, :, :, None] * jnp.transpose(phase, (1, 0, 2))[:, :, None, None, :])
    l2 = jnp.transpose(l2, (0, 2, 3, 1, 4)).astype(jnp.bfloat16)
    folded = jnp.einsum("raqsk,skn->raqn", l2, p2, preferred_element_type=jnp.float32).astype(jnp.bfloat16)
    folded = folded.reshape(NF, row_cells, q_cells, S, 2 * S)

    j_index = resid[:, None] + NF * (jnp.arange(j_len, dtype=jnp.int32)[None, :] - j_len // 2)
    coarse = jnp.arange(q_cells, dtype=jnp.int32) * S
    fine = jnp.arange(S, dtype=jnp.int32)
    ca, sa = cos_sin_f32(jnp.mod(coarse[None, :, None] * (spacing * j_index[:, None, :]), G))
    cb, sb = cos_sin_f32(jnp.mod(fine[None, :, None] * (spacing * j_index[:, None, :]), G))
    c1 = (ca[:, :, None, :] * cb[:, None, :, :] - sa[:, :, None, :] * sb[:, None, :, :]).astype(jnp.bfloat16)
    s1 = (sa[:, :, None, :] * cb[:, None, :, :] + ca[:, :, None, :] * sb[:, None, :, :]).astype(jnp.bfloat16)
    c1 = c1.reshape(NF, q_cells, 1, S, 1, j_len)
    s1 = s1.reshape(NF, q_cells, 1, S, 1, j_len)
    ri_in = jnp.arange(2, dtype=jnp.int32).reshape(1, 1, 2, 1, 1, 1)
    ri_out = jnp.arange(2, dtype=jnp.int32).reshape(1, 1, 1, 1, 2, 1)
    w1 = jnp.where(ri_in == ri_out, c1, jnp.where(ri_in == 0, s1, -s1))
    w1 = w1.reshape(NF, q_cells, 2 * S, 2 * j_len)
    transformed = jnp.einsum("raqxk,rqkn->raxn", folded, w1, preferred_element_type=jnp.float32)
    transformed = transformed.astype(jnp.bfloat16).reshape(NF, slab_rows, 2, j_len)

    l_index = jnp.arange(P_SIZE, dtype=jnp.int32) - P_SIZE // 2
    row_base = (tile_index * slab_rows - G // 2) + jnp.arange(row_cells, dtype=jnp.int32) * S
    ca, sa = cos_sin_f32(phase_index(row_base, l_index))
    cb, sb = cos_sin_f32(phase_index(fine, l_index))
    c2 = (ca[:, None, :] * cb[None, :, :] - sa[:, None, :] * sb[None, :, :]).astype(jnp.bfloat16)
    s2 = (sa[:, None, :] * cb[None, :, :] + ca[:, None, :] * sb[None, :, :]).astype(jnp.bfloat16)
    c2 = c2.reshape(slab_rows, P_SIZE)
    s2 = s2.reshape(slab_rows, P_SIZE)
    e2 = jnp.stack([c2, -s2])
    partial = jnp.einsum("iul,ruij->lrj", e2, transformed, preferred_element_type=jnp.float32)
    chan_count = lax.axis_size("chan")
    partial = partial.reshape(chan_count, P_SIZE // chan_count, NF, j_len)
    partial = lax.all_to_all(partial.astype(jnp.bfloat16), "chan", split_axis=0, concat_axis=0, tiled=True)
    partial = jnp.sum(partial.astype(jnp.float32), axis=0)
    partial = partial.reshape(P_SIZE // chan_count, NF, tile_count, j_len // tile_count)
    partial = jnp.transpose(partial, (2, 0, 1, 3))
    partial = lax.all_to_all(partial.astype(jnp.bfloat16), "tile", split_axis=0, concat_axis=0, tiled=True)
    partial = jnp.sum(partial.astype(jnp.float32), axis=0)
    out = jnp.transpose(partial, (0, 2, 1))
    return out.reshape(out.shape[0], -1) * (1.0 / G)


def solution(mesh):
    placed = (
        P("chan", "tile", None),
        P("chan", None, None, None, None),
        P("chan", "tile", None),
        P("chan", "tile"),
        P("chan", "tile"),
    )
    return jax.shard_map(
        local, mesh=mesh, in_specs=placed, out_specs=P("chan", "tile"), check_vma=False
    )
```

```python
import math

import jax
import jax.numpy as jnp
from jax import lax
from jax.sharding import PartitionSpec as P
from jax.experimental import pallas as pl
from jax.experimental.pallas import tpu as pltpu

G = 8192
S = 64
NW = 32
P_SIZE = 1024
NF = 8


def block_patches(samples, kernel_rows):
    sample_count = samples.shape[1] // 2
    support = kernel_rows.shape[3] // 2
    vis_real = samples[:, :sample_count, None]
    vis_imag = samples[:, sample_count:, None]
    kern_real = kernel_rows[:, 0].astype(jnp.float32)
    kern_imag = kernel_rows[:, 1].astype(jnp.float32)
    full_real = (vis_real * kern_real - vis_imag * kern_imag).astype(jnp.bfloat16)
    full_imag = (vis_real * kern_imag + vis_imag * kern_real).astype(jnp.bfloat16)
    weighted_real = full_real[:, :, support:]
    weighted_imag = full_imag[:, :, support:]
    v_weighted = jnp.stack(
        [
            jnp.concatenate([weighted_real, weighted_imag], axis=-1),
            jnp.concatenate([-weighted_imag, weighted_real], axis=-1),
        ],
        1,
    )
    patch = jnp.einsum("bpkx,bpkn->bxn", kernel_rows, v_weighted, preferred_element_type=jnp.float32)
    return patch[:, :support, :]


PATCH_CHUNK = 128


def patch_kernel(plane_ref, samples_ref, u_ref, v_ref, out_ref):
    base = pl.program_id(0) * PATCH_CHUNK
    lane = lax.broadcasted_iota(jnp.int32, (S, 2 * S), 1)
    low = lane < S
    sign = jnp.where(low, -1.0, 1.0).astype(jnp.float32)
    for j in range(PATCH_CHUNK):
        w = plane_ref[base + j]
        column = samples_ref[:, j : j + 1]
        vis_real = column[:S]
        vis_imag = column[S:]
        kern_real = v_ref[w, 0].astype(jnp.float32)
        kern_imag = v_ref[w, 1].astype(jnp.float32)
        w_real = (vis_real * kern_real - vis_imag * kern_imag).astype(jnp.bfloat16).astype(jnp.float32)
        w_imag = (vis_real * kern_imag + vis_imag * kern_real).astype(jnp.bfloat16).astype(jnp.float32)
        top = jnp.where(low, pltpu.roll(w_real, S, 1), w_imag)
        bottom = jnp.where(low, -pltpu.roll(w_imag, S, 1), w_real)
        rhs = jnp.concatenate([top, bottom], axis=0).astype(jnp.bfloat16)
        patch = jnp.dot(u_ref[w], rhs, preferred_element_type=jnp.float32)
        out_ref[j, 0] = patch.astype(jnp.bfloat16)
        out_ref[j, 1] = (pltpu.roll(patch, S, 1) * sign).astype(jnp.bfloat16)


def patches_rotated(samples, planes, kernel_set):
    slots = samples.shape[0]
    u_kernel = jnp.transpose(kernel_set[:, :, :, :S], (0, 3, 1, 2)).reshape(NW, S, 2 * S)
    grid_spec = pltpu.PrefetchScalarGridSpec(
        num_scalar_prefetch=1,
        grid=(slots // PATCH_CHUNK,),
        in_specs=[
            pl.BlockSpec((2 * S, PATCH_CHUNK), lambda i, p: (0, i)),
            pl.BlockSpec((NW, S, 2 * S), lambda i, p: (0, 0, 0)),
            pl.BlockSpec((NW, 2, S, 2 * S), lambda i, p: (0, 0, 0, 0)),
        ],
        out_specs=pl.BlockSpec((PATCH_CHUNK, 2, S, 2 * S), lambda i, p: (i, 0, 0, 0)),
    )
    return pl.pallas_call(
        patch_kernel,
        grid_spec=grid_spec,
        out_shape=jax.ShapeDtypeStruct((slots, 2, S, 2 * S), jnp.bfloat16),
        cost_estimate=pl.CostEstimate(
            flops=2 * slots * S * 2 * S * 2 * S, transcendentals=0, bytes_accessed=slots * 2 * S * 2 * S * 2 * 2
        ),
    )(planes, jnp.transpose(samples), u_kernel, kernel_set)


def phase_index(rows, cols):
    spacing = G // P_SIZE - 1
    return jnp.mod(rows[:, None] * (spacing * cols[None, :]), G)


def cos_sin_f32(index):
    angle = index.astype(jnp.float32) * (2.0 * math.pi / G)
    return jnp.cos(angle), jnp.sin(angle)


def local(visibilities, kernels, destination, cell, plane):
    tile_count = lax.axis_size("tile")
    tile_index = lax.axis_index("tile")
    samples = visibilities[0]
    kernel_set = kernels[0]
    owners = destination[0, :, 0]
    blocks = samples.shape[0]
    capacity = 3 * blocks // tile_count
    spacing = G // P_SIZE - 1

    counts = jnp.sum(
        (owners[:, None] == jnp.arange(tile_count, dtype=jnp.int32)[None, :]).astype(jnp.int32), axis=0
    )
    first = jnp.cumsum(counts) - counts
    order = jnp.argsort(owners, stable=True).astype(jnp.int32)
    slot = jnp.arange(capacity, dtype=jnp.int32)
    valid = slot[None, :] < counts[:, None]
    src = order[jnp.clip(first[:, None] + slot[None, :], 0, blocks - 1)]
    packed_meta = cell[0] * NW + plane[0]
    send_samples = jnp.where(valid[:, :, None], samples[src], 0.0)
    send_meta = jnp.where(valid, packed_meta[src], 0)
    arrived = lax.all_to_all(send_samples, "tile", split_axis=0, concat_axis=0, tiled=True)
    arrived_meta = lax.all_to_all(send_meta, "tile", split_axis=0, concat_axis=0, tiled=True)
    slot_total = tile_count * capacity
    arrived = arrived.reshape(slot_total, samples.shape[1])
    arrived_meta = arrived_meta.reshape(slot_total)

    slab_rows = G // tile_count
    row_cells = slab_rows // S
    cell_cols = G // S
    q_len = G // NF
    q_cells = q_len // S
    j_len = P_SIZE // NF

    cell_r = arrived_meta // NW
    plane_r = arrived_meta % NW
    p2 = patches_rotated(arrived, plane_r, kernel_set).reshape(slot_total, 2, S * 2 * S)

    a_s = cell_r // cell_cols
    cc_s = cell_r % cell_cols
    p_s = cc_s // q_cells
    qc_s = cc_s % q_cells
    resid = jnp.arange(NF, dtype=jnp.int32)
    ph_index = jnp.mod(spacing * (p_s[:, None] - NF // 2) * resid[None, :], NF)
    ph_angle = ph_index.astype(jnp.float32) * (2.0 * math.pi / NF)
    phase = jnp.stack([jnp.cos(ph_angle), jnp.sin(ph_angle)], axis=-1)
    place = (a_s[:, None] == jnp.arange(row_cells, dtype=jnp.int32)[None, :])[:, :, None] & (
        qc_s[:, None] == jnp.arange(q_cells, dtype=jnp.int32)[None, :]
    )[:, None, :]
    l2 = (place.astype(jnp.float32)[None, :, :, :, None] * jnp.transpose(phase, (1, 0, 2))[:, :, None, None, :])
    l2 = jnp.transpose(l2, (0, 2, 3, 1, 4)).astype(jnp.bfloat16)
    folded = jnp.einsum("raqsk,skn->raqn", l2, p2, preferred_element_type=jnp.float32).astype(jnp.bfloat16)
    folded = folded.reshape(NF, row_cells, q_cells, S, 2 * S)

    j_index = resid[:, None] + NF * (jnp.arange(j_len, dtype=jnp.int32)[None, :] - j_len // 2)
    coarse = jnp.arange(q_cells, dtype=jnp.int32) * S
    fine = jnp.arange(S, dtype=jnp.int32)
    ca, sa = cos_sin_f32(jnp.mod(coarse[None, :, None] * (spacing * j_index[:, None, :]), G))
    cb, sb = cos_sin_f32(jnp.mod(fine[None, :, None] * (spacing * j_index[:, None, :]), G))
    c1 = (ca[:, :, None, :] * cb[:, None, :, :] - sa[:, :, None, :] * sb[:, None, :, :]).astype(jnp.bfloat16)
    s1 = (sa[:, :, None, :] * cb[:, None, :, :] + ca[:, :, None, :] * sb[:, None, :, :]).astype(jnp.bfloat16)
    c1 = c1.reshape(NF, q_cells, 1, S, 1, j_len)
    s1 = s1.reshape(NF, q_cells, 1, S, 1, j_len)
    ri_in = jnp.arange(2, dtype=jnp.int32).reshape(1, 1, 2, 1, 1, 1)
    ri_out = jnp.arange(2, dtype=jnp.int32).reshape(1, 1, 1, 1, 2, 1)
    w1 = jnp.where(ri_in == ri_out, c1, jnp.where(ri_in == 0, s1, -s1))
    w1 = w1.reshape(NF, q_cells, 2 * S, 2 * j_len)
    transformed = jnp.einsum("raqxk,rqkn->raxn", folded, w1, preferred_element_type=jnp.float32)
    transformed = transformed.astype(jnp.bfloat16).reshape(NF, slab_rows, 2, j_len)

    l_index = jnp.arange(P_SIZE, dtype=jnp.int32) - P_SIZE // 2
    row_base = (tile_index * slab_rows - G // 2) + jnp.arange(row_cells, dtype=jnp.int32) * S
    ca, sa = cos_sin_f32(phase_index(row_base, l_index))
    cb, sb = cos_sin_f32(phase_index(fine, l_index))
    c2 = (ca[:, None, :] * cb[None, :, :] - sa[:, None, :] * sb[None, :, :]).astype(jnp.bfloat16)
    s2 = (sa[:, None, :] * cb[None, :, :] + ca[:, None, :] * sb[None, :, :]).astype(jnp.bfloat16)
    c2 = c2.reshape(slab_rows, P_SIZE)
    s2 = s2.reshape(slab_rows, P_SIZE)
    e2 = jnp.stack([c2, -s2])
    partial = jnp.einsum("iul,ruij->lrj", e2, transformed, preferred_element_type=jnp.float32)
    chan_count = lax.axis_size("chan")
    partial = partial.reshape(chan_count, P_SIZE // chan_count, NF, j_len)
    partial = lax.all_to_all(partial.astype(jnp.bfloat16), "chan", split_axis=0, concat_axis=0, tiled=True)
    partial = jnp.sum(partial.astype(jnp.float32), axis=0)
    partial = partial.reshape(P_SIZE // chan_count, NF, tile_count, j_len // tile_count)
    partial = jnp.transpose(partial, (2, 0, 1, 3))
    partial = lax.all_to_all(partial.astype(jnp.bfloat16), "tile", split_axis=0, concat_axis=0, tiled=True)
    partial = jnp.sum(partial.astype(jnp.float32), axis=0)
    out = jnp.transpose(partial, (0, 2, 1))
    return out.reshape(out.shape[0], -1) * (1.0 / G)


def solution(mesh):
    placed = (
        P("chan", "tile", None),
        P("chan", None, None, None, None),
        P("chan", "tile", None),
        P("chan", "tile"),
        P("chan", "tile"),
    )
    return jax.shard_map(
        local, mesh=mesh, in_specs=placed, out_specs=P("chan", "tile"), check_vma=False
    )
```

```python
import math

import jax
import jax.numpy as jnp
from jax import lax
from jax.sharding import PartitionSpec as P
from jax.experimental import pallas as pl
from jax.experimental.pallas import tpu as pltpu

G = 8192
S = 64
NW = 32
P_SIZE = 1024
NF = 8


def block_patches(samples, kernel_rows):
    sample_count = samples.shape[1] // 2
    support = kernel_rows.shape[3] // 2
    vis_real = samples[:, :sample_count, None]
    vis_imag = samples[:, sample_count:, None]
    kern_real = kernel_rows[:, 0].astype(jnp.float32)
    kern_imag = kernel_rows[:, 1].astype(jnp.float32)
    full_real = (vis_real * kern_real - vis_imag * kern_imag).astype(jnp.bfloat16)
    full_imag = (vis_real * kern_imag + vis_imag * kern_real).astype(jnp.bfloat16)
    weighted_real = full_real[:, :, support:]
    weighted_imag = full_imag[:, :, support:]
    v_weighted = jnp.stack(
        [
            jnp.concatenate([weighted_real, weighted_imag], axis=-1),
            jnp.concatenate([-weighted_imag, weighted_real], axis=-1),
        ],
        1,
    )
    patch = jnp.einsum("bpkx,bpkn->bxn", kernel_rows, v_weighted, preferred_element_type=jnp.float32)
    return patch[:, :support, :]


PATCH_CHUNK = 128


def patch_kernel(plane_ref, samples_ref, u_ref, v_ref, out_ref):
    base = pl.program_id(0) * PATCH_CHUNK
    for j in range(PATCH_CHUNK):
        w = plane_ref[base + j]
        column = samples_ref[:, j : j + 1]
        vis_real = column[:S]
        vis_imag = column[S:]
        first = v_ref[w, 0].astype(jnp.float32)
        second = v_ref[w, 1].astype(jnp.float32)
        top = (vis_real * first + vis_imag * second).astype(jnp.bfloat16)
        bottom = (vis_real * second - vis_imag * first).astype(jnp.bfloat16)
        rhs = jnp.concatenate(
            [jnp.concatenate([top, bottom], axis=1), jnp.concatenate([bottom, -top], axis=1)], axis=0
        )
        both = jnp.dot(u_ref[w], rhs, preferred_element_type=jnp.float32)
        out_ref[j, 0] = both[:, : 2 * S].astype(jnp.bfloat16)
        out_ref[j, 1] = both[:, 2 * S :].astype(jnp.bfloat16)


def patches_rotated(samples, planes, kernel_set):
    slots = samples.shape[0]
    u_kernel = jnp.transpose(kernel_set[:, :, :, :S], (0, 3, 1, 2)).reshape(NW, S, 2 * S)
    v_real = kernel_set[:, 0, :, S:]
    v_imag = kernel_set[:, 1, :, S:]
    v_parts = jnp.stack(
        [jnp.concatenate([v_real, v_imag], axis=-1), jnp.concatenate([-v_imag, v_real], axis=-1)], axis=1
    )
    grid_spec = pltpu.PrefetchScalarGridSpec(
        num_scalar_prefetch=1,
        grid=(slots // PATCH_CHUNK,),
        in_specs=[
            pl.BlockSpec((2 * S, PATCH_CHUNK), lambda i, p: (0, i)),
            pl.BlockSpec((NW, S, 2 * S), lambda i, p: (0, 0, 0)),
            pl.BlockSpec((NW, 2, S, 2 * S), lambda i, p: (0, 0, 0, 0)),
        ],
        out_specs=pl.BlockSpec((PATCH_CHUNK, 2, S, 2 * S), lambda i, p: (i, 0, 0, 0)),
    )
    return pl.pallas_call(
        patch_kernel,
        grid_spec=grid_spec,
        out_shape=jax.ShapeDtypeStruct((slots, 2, S, 2 * S), jnp.bfloat16),
        cost_estimate=pl.CostEstimate(
            flops=2 * slots * S * 2 * S * 4 * S, transcendentals=0, bytes_accessed=slots * 2 * S * 2 * S * 2 * 2
        ),
    )(planes, jnp.transpose(samples), u_kernel, v_parts)


def phase_index(rows, cols):
    spacing = G // P_SIZE - 1
    return jnp.mod(rows[:, None] * (spacing * cols[None, :]), G)


def cos_sin_f32(index):
    angle = index.astype(jnp.float32) * (2.0 * math.pi / G)
    return jnp.cos(angle), jnp.sin(angle)


def local(visibilities, kernels, destination, cell, plane):
    tile_count = lax.axis_size("tile")
    tile_index = lax.axis_index("tile")
    samples = visibilities[0]
    kernel_set = kernels[0]
    owners = destination[0, :, 0]
    blocks = samples.shape[0]
    capacity = 3 * blocks // tile_count
    spacing = G // P_SIZE - 1

    counts = jnp.sum(
        (owners[:, None] == jnp.arange(tile_count, dtype=jnp.int32)[None, :]).astype(jnp.int32), axis=0
    )
    first = jnp.cumsum(counts) - counts
    order = jnp.argsort(owners, stable=True).astype(jnp.int32)
    slot = jnp.arange(capacity, dtype=jnp.int32)
    valid = slot[None, :] < counts[:, None]
    src = order[jnp.clip(first[:, None] + slot[None, :], 0, blocks - 1)]
    packed_meta = cell[0] * NW + plane[0]
    send_samples = jnp.where(valid[:, :, None], samples[src], 0.0)
    send_meta = jnp.where(valid, packed_meta[src], 0)
    arrived = lax.all_to_all(send_samples, "tile", split_axis=0, concat_axis=0, tiled=True)
    arrived_meta = lax.all_to_all(send_meta, "tile", split_axis=0, concat_axis=0, tiled=True)
    slot_total = tile_count * capacity
    arrived = arrived.reshape(slot_total, samples.shape[1])
    arrived_meta = arrived_meta.reshape(slot_total)

    slab_rows = G // tile_count
    row_cells = slab_rows // S
    cell_cols = G // S
    q_len = G // NF
    q_cells = q_len // S
    j_len = P_SIZE // NF

    cell_r = arrived_meta // NW
    plane_r = arrived_meta % NW
    p2 = patches_rotated(arrived, plane_r, kernel_set).reshape(slot_total, 2, S * 2 * S)

    a_s = cell_r // cell_cols
    cc_s = cell_r % cell_cols
    p_s = cc_s // q_cells
    qc_s = cc_s % q_cells
    resid = jnp.arange(NF, dtype=jnp.int32)
    ph_index = jnp.mod(spacing * (p_s[:, None] - NF // 2) * resid[None, :], NF)
    ph_angle = ph_index.astype(jnp.float32) * (2.0 * math.pi / NF)
    phase = jnp.stack([jnp.cos(ph_angle), jnp.sin(ph_angle)], axis=-1)
    place = (a_s[:, None] == jnp.arange(row_cells, dtype=jnp.int32)[None, :])[:, :, None] & (
        qc_s[:, None] == jnp.arange(q_cells, dtype=jnp.int32)[None, :]
    )[:, None, :]
    l2 = (place.astype(jnp.float32)[None, :, :, :, None] * jnp.transpose(phase, (1, 0, 2))[:, :, None, None, :])
    l2 = jnp.transpose(l2, (0, 2, 3, 1, 4)).astype(jnp.bfloat16)
    folded = jnp.einsum("raqsk,skn->raqn", l2, p2, preferred_element_type=jnp.float32).astype(jnp.bfloat16)
    folded = folded.reshape(NF, row_cells, q_cells, S, 2 * S)

    j_index = resid[:, None] + NF * (jnp.arange(j_len, dtype=jnp.int32)[None, :] - j_len // 2)
    coarse = jnp.arange(q_cells, dtype=jnp.int32) * S
    fine = jnp.arange(S, dtype=jnp.int32)
    ca, sa = cos_sin_f32(jnp.mod(coarse[None, :, None] * (spacing * j_index[:, None, :]), G))
    cb, sb = cos_sin_f32(jnp.mod(fine[None, :, None] * (spacing * j_index[:, None, :]), G))
    ca = jnp.tile(ca, (1, 1, 2))[:, :, None, :]
    sa = jnp.tile(sa, (1, 1, 2))[:, :, None, :]
    cb = jnp.tile(cb, (1, 2, 2))[:, None, :, :]
    sb = jnp.tile(sb, (1, 2, 2))[:, None, :, :]
    c1 = (ca * cb - sa * sb).astype(jnp.bfloat16)
    s1 = (sa * cb + ca * sb).astype(jnp.bfloat16)
    ri_in = lax.broadcasted_iota(jnp.int32, (1, 1, 2 * S, 2 * j_len), 2) // S
    ri_out = lax.broadcasted_iota(jnp.int32, (1, 1, 2 * S, 2 * j_len), 3) // j_len
    w1 = jnp.where(ri_in == ri_out, c1, jnp.where(ri_in == 0, s1, -s1))
    transformed = jnp.einsum("raqxk,rqkn->raxn", folded, w1, preferred_element_type=jnp.float32)
    transformed = transformed.astype(jnp.bfloat16).reshape(NF, slab_rows, 2, j_len)

    l_index = jnp.arange(P_SIZE, dtype=jnp.int32) - P_SIZE // 2
    row_base = (tile_index * slab_rows - G // 2) + jnp.arange(row_cells, dtype=jnp.int32) * S
    ca, sa = cos_sin_f32(phase_index(row_base, l_index))
    cb, sb = cos_sin_f32(phase_index(fine, l_index))
    c2 = (ca[:, None, :] * cb[None, :, :] - sa[:, None, :] * sb[None, :, :]).astype(jnp.bfloat16)
    s2 = (sa[:, None, :] * cb[None, :, :] + ca[:, None, :] * sb[None, :, :]).astype(jnp.bfloat16)
    c2 = c2.reshape(slab_rows, P_SIZE)
    s2 = s2.reshape(slab_rows, P_SIZE)
    e2 = jnp.stack([c2, -s2])
    partial = jnp.einsum("iul,ruij->lrj", e2, transformed, preferred_element_type=jnp.float32)
    chan_count = lax.axis_size("chan")
    partial = partial.reshape(chan_count, P_SIZE // chan_count, NF, j_len)
    partial = lax.all_to_all(partial.astype(jnp.bfloat16), "chan", split_axis=0, concat_axis=0, tiled=True)
    partial = jnp.sum(partial.astype(jnp.float32), axis=0)
    partial = partial.reshape(P_SIZE // chan_count, NF, tile_count, j_len // tile_count)
    partial = jnp.transpose(partial, (2, 0, 1, 3))
    partial = lax.all_to_all(partial.astype(jnp.bfloat16), "tile", split_axis=0, concat_axis=0, tiled=True)
    partial = jnp.sum(partial.astype(jnp.float32), axis=0)
    out = jnp.transpose(partial, (0, 2, 1))
    return out.reshape(out.shape[0], -1) * (1.0 / G)


def solution(mesh):
    placed = (
        P("chan", "tile", None),
        P("chan", None, None, None, None),
        P("chan", "tile", None),
        P("chan", "tile"),
        P("chan", "tile"),
    )
    return jax.shard_map(
        local, mesh=mesh, in_specs=placed, out_specs=P("chan", "tile"), check_vma=False
    )
```

```python
import math

import jax
import jax.numpy as jnp
from jax import lax
from jax.sharding import PartitionSpec as P
from jax.experimental import pallas as pl
from jax.experimental.pallas import tpu as pltpu

G = 8192
S = 64
NW = 32
P_SIZE = 1024
NF = 8


def block_patches(samples, kernel_rows):
    sample_count = samples.shape[1] // 2
    support = kernel_rows.shape[3] // 2
    vis_real = samples[:, :sample_count, None]
    vis_imag = samples[:, sample_count:, None]
    kern_real = kernel_rows[:, 0].astype(jnp.float32)
    kern_imag = kernel_rows[:, 1].astype(jnp.float32)
    full_real = (vis_real * kern_real - vis_imag * kern_imag).astype(jnp.bfloat16)
    full_imag = (vis_real * kern_imag + vis_imag * kern_real).astype(jnp.bfloat16)
    weighted_real = full_real[:, :, support:]
    weighted_imag = full_imag[:, :, support:]
    v_weighted = jnp.stack(
        [
            jnp.concatenate([weighted_real, weighted_imag], axis=-1),
            jnp.concatenate([-weighted_imag, weighted_real], axis=-1),
        ],
        1,
    )
    patch = jnp.einsum("bpkx,bpkn->bxn", kernel_rows, v_weighted, preferred_element_type=jnp.float32)
    return patch[:, :support, :]


PATCH_CHUNK = 128


def patch_kernel(plane_ref, samples_ref, u_ref, v_ref, out_ref):
    base = pl.program_id(0) * PATCH_CHUNK
    for j in range(PATCH_CHUNK):
        w = plane_ref[base + j]
        column = samples_ref[:, j : j + 1]
        vis_real = column[:S]
        vis_imag = column[S:]
        first = v_ref[w, 0].astype(jnp.float32)
        second = v_ref[w, 1].astype(jnp.float32)
        top = (vis_real * first + vis_imag * second).astype(jnp.bfloat16)
        bottom = (vis_real * second - vis_imag * first).astype(jnp.bfloat16)
        rhs = jnp.concatenate(
            [jnp.concatenate([top, bottom], axis=1), jnp.concatenate([bottom, -top], axis=1)], axis=0
        )
        both = jnp.dot(u_ref[w], rhs, preferred_element_type=jnp.float32)
        out_ref[j, 0] = both[:, : 2 * S].astype(jnp.bfloat16)
        out_ref[j, 1] = both[:, 2 * S :].astype(jnp.bfloat16)


def patches_rotated(samples, planes, kernel_set):
    slots = samples.shape[0]
    u_kernel = jnp.transpose(kernel_set[:, :, :, :S], (0, 3, 1, 2)).reshape(NW, S, 2 * S)
    v_real = kernel_set[:, 0, :, S:]
    v_imag = kernel_set[:, 1, :, S:]
    v_parts = jnp.stack(
        [jnp.concatenate([v_real, v_imag], axis=-1), jnp.concatenate([-v_imag, v_real], axis=-1)], axis=1
    )
    grid_spec = pltpu.PrefetchScalarGridSpec(
        num_scalar_prefetch=1,
        grid=(slots // PATCH_CHUNK,),
        in_specs=[
            pl.BlockSpec((2 * S, PATCH_CHUNK), lambda i, p: (0, i)),
            pl.BlockSpec((NW, S, 2 * S), lambda i, p: (0, 0, 0)),
            pl.BlockSpec((NW, 2, S, 2 * S), lambda i, p: (0, 0, 0, 0)),
        ],
        out_specs=pl.BlockSpec((PATCH_CHUNK, 2, S, 2 * S), lambda i, p: (i, 0, 0, 0)),
    )
    return pl.pallas_call(
        patch_kernel,
        grid_spec=grid_spec,
        out_shape=jax.ShapeDtypeStruct((slots, 2, S, 2 * S), jnp.bfloat16),
        cost_estimate=pl.CostEstimate(
            flops=2 * slots * S * 2 * S * 4 * S, transcendentals=0, bytes_accessed=slots * 2 * S * 2 * S * 2 * 2
        ),
    )(planes, jnp.transpose(samples), u_kernel, v_parts)


def phase_index(rows, cols):
    spacing = G // P_SIZE - 1
    return jnp.mod(rows[:, None] * (spacing * cols[None, :]), G)


def cos_sin_f32(index):
    angle = index.astype(jnp.float32) * (2.0 * math.pi / G)
    return jnp.cos(angle), jnp.sin(angle)


def local(visibilities, kernels, destination, cell, plane):
    tile_count = lax.axis_size("tile")
    tile_index = lax.axis_index("tile")
    samples = visibilities[0]
    kernel_set = kernels[0]
    owners = destination[0, :, 0]
    blocks = samples.shape[0]
    capacity = 3 * blocks // tile_count
    spacing = G // P_SIZE - 1

    counts = jnp.sum(
        (owners[:, None] == jnp.arange(tile_count, dtype=jnp.int32)[None, :]).astype(jnp.int32), axis=0
    )
    first = jnp.cumsum(counts) - counts
    order = jnp.argsort(owners, stable=True).astype(jnp.int32)
    slot = jnp.arange(capacity, dtype=jnp.int32)
    valid = slot[None, :] < counts[:, None]
    src = order[jnp.clip(first[:, None] + slot[None, :], 0, blocks - 1)]
    packed_meta = cell[0] * NW + plane[0]
    send_samples = jnp.where(valid[:, :, None], samples[src], 0.0)
    send_meta = jnp.where(valid, packed_meta[src], 0).astype(jnp.float32)
    meta_row = jnp.pad(send_meta, ((0, 0), (0, samples.shape[1] - capacity)))[:, None, :]
    arrived = lax.all_to_all(
        jnp.concatenate([send_samples, meta_row], axis=1), "tile", split_axis=0, concat_axis=0, tiled=True
    )
    slot_total = tile_count * capacity
    arrived_meta = arrived[:, capacity, :capacity].astype(jnp.int32).reshape(slot_total)
    arrived = arrived[:, :capacity, :].reshape(slot_total, samples.shape[1])

    slab_rows = G // tile_count
    row_cells = slab_rows // S
    cell_cols = G // S
    q_len = G // NF
    q_cells = q_len // S
    j_len = P_SIZE // NF

    cell_r = arrived_meta // NW
    plane_r = arrived_meta % NW
    p2 = patches_rotated(arrived, plane_r, kernel_set).reshape(slot_total, 2, S * 2 * S)

    a_s = cell_r // cell_cols
    cc_s = cell_r % cell_cols
    p_s = cc_s // q_cells
    qc_s = cc_s % q_cells
    resid = jnp.arange(NF, dtype=jnp.int32)
    ph_index = jnp.mod(spacing * (p_s[:, None] - NF // 2) * resid[None, :], NF)
    ph_angle = ph_index.astype(jnp.float32) * (2.0 * math.pi / NF)
    phase = jnp.stack([jnp.cos(ph_angle), jnp.sin(ph_angle)], axis=-1)
    place = (a_s[:, None] == jnp.arange(row_cells, dtype=jnp.int32)[None, :])[:, :, None] & (
        qc_s[:, None] == jnp.arange(q_cells, dtype=jnp.int32)[None, :]
    )[:, None, :]
    l2 = (place.astype(jnp.float32)[None, :, :, :, None] * jnp.transpose(phase, (1, 0, 2))[:, :, None, None, :])
    l2 = jnp.transpose(l2, (0, 2, 3, 1, 4)).astype(jnp.bfloat16)
    folded = jnp.einsum("raqsk,skn->raqn", l2, p2, preferred_element_type=jnp.float32).astype(jnp.bfloat16)
    folded = folded.reshape(NF, row_cells, q_cells, S, 2 * S)

    j_index = resid[:, None] + NF * (jnp.arange(j_len, dtype=jnp.int32)[None, :] - j_len // 2)
    coarse = jnp.arange(q_cells, dtype=jnp.int32) * S
    fine = jnp.arange(S, dtype=jnp.int32)
    ca, sa = cos_sin_f32(jnp.mod(coarse[None, :, None] * (spacing * j_index[:, None, :]), G))
    cb, sb = cos_sin_f32(jnp.mod(fine[None, :, None] * (spacing * j_index[:, None, :]), G))
    ca = jnp.tile(ca, (1, 1, 2))[:, :, None, :]
    sa = jnp.tile(sa, (1, 1, 2))[:, :, None, :]
    cb = jnp.tile(cb, (1, 2, 2))[:, None, :, :]
    sb = jnp.tile(sb, (1, 2, 2))[:, None, :, :]
    c1 = (ca * cb - sa * sb).astype(jnp.bfloat16)
    s1 = (sa * cb + ca * sb).astype(jnp.bfloat16)
    ri_in = lax.broadcasted_iota(jnp.int32, (1, 1, 2 * S, 2 * j_len), 2) // S
    ri_out = lax.broadcasted_iota(jnp.int32, (1, 1, 2 * S, 2 * j_len), 3) // j_len
    w1 = jnp.where(ri_in == ri_out, c1, jnp.where(ri_in == 0, s1, -s1))
    transformed = jnp.einsum("raqxk,rqkn->raxn", folded, w1, preferred_element_type=jnp.float32)
    transformed = transformed.astype(jnp.bfloat16).reshape(NF, slab_rows, 2, j_len)

    l_index = jnp.arange(P_SIZE, dtype=jnp.int32) - P_SIZE // 2
    row_base = (tile_index * slab_rows - G // 2) + jnp.arange(row_cells, dtype=jnp.int32) * S
    ca, sa = cos_sin_f32(phase_index(row_base, l_index))
    cb, sb = cos_sin_f32(phase_index(fine, l_index))
    c2 = (ca[:, None, :] * cb[None, :, :] - sa[:, None, :] * sb[None, :, :]).astype(jnp.bfloat16)
    s2 = (sa[:, None, :] * cb[None, :, :] + ca[:, None, :] * sb[None, :, :]).astype(jnp.bfloat16)
    c2 = c2.reshape(slab_rows, P_SIZE)
    s2 = s2.reshape(slab_rows, P_SIZE)
    e2 = jnp.stack([c2, -s2])
    partial = jnp.einsum("iul,ruij->lrj", e2, transformed, preferred_element_type=jnp.float32)
    chan_count = lax.axis_size("chan")
    partial = partial.reshape(chan_count, P_SIZE // chan_count, NF, j_len)
    partial = lax.all_to_all(partial.astype(jnp.bfloat16), "chan", split_axis=0, concat_axis=0, tiled=True)
    partial = jnp.sum(partial.astype(jnp.float32), axis=0)
    partial = partial.reshape(P_SIZE // chan_count, NF, tile_count, j_len // tile_count)
    partial = jnp.transpose(partial, (2, 0, 1, 3))
    partial = lax.all_to_all(partial.astype(jnp.bfloat16), "tile", split_axis=0, concat_axis=0, tiled=True)
    partial = jnp.sum(partial.astype(jnp.float32), axis=0)
    out = jnp.transpose(partial, (0, 2, 1))
    return out.reshape(out.shape[0], -1) * (1.0 / G)


def solution(mesh):
    placed = (
        P("chan", "tile", None),
        P("chan", None, None, None, None),
        P("chan", "tile", None),
        P("chan", "tile"),
        P("chan", "tile"),
    )
    return jax.shard_map(
        local, mesh=mesh, in_specs=placed, out_specs=P("chan", "tile"), check_vma=False
    )
```

```python
import math

import jax
import jax.numpy as jnp
from jax import lax
from jax.sharding import PartitionSpec as P
from jax.experimental import pallas as pl
from jax.experimental.pallas import tpu as pltpu

G = 8192
S = 64
NW = 32
P_SIZE = 1024
NF = 8


def block_patches(samples, kernel_rows):
    sample_count = samples.shape[1] // 2
    support = kernel_rows.shape[3] // 2
    vis_real = samples[:, :sample_count, None]
    vis_imag = samples[:, sample_count:, None]
    kern_real = kernel_rows[:, 0].astype(jnp.float32)
    kern_imag = kernel_rows[:, 1].astype(jnp.float32)
    full_real = (vis_real * kern_real - vis_imag * kern_imag).astype(jnp.bfloat16)
    full_imag = (vis_real * kern_imag + vis_imag * kern_real).astype(jnp.bfloat16)
    weighted_real = full_real[:, :, support:]
    weighted_imag = full_imag[:, :, support:]
    v_weighted = jnp.stack(
        [
            jnp.concatenate([weighted_real, weighted_imag], axis=-1),
            jnp.concatenate([-weighted_imag, weighted_real], axis=-1),
        ],
        1,
    )
    patch = jnp.einsum("bpkx,bpkn->bxn", kernel_rows, v_weighted, preferred_element_type=jnp.float32)
    return patch[:, :support, :]


PATCH_CHUNK = 128


def patch_kernel(plane_ref, samples_ref, u_ref, v_ref, out_ref):
    base = pl.program_id(0) * PATCH_CHUNK
    for j in range(PATCH_CHUNK):
        w = plane_ref[base + j]
        column = samples_ref[:, j : j + 1]
        vis_real = column[:S]
        vis_imag = column[S:]
        first = v_ref[w, 0].astype(jnp.float32)
        second = v_ref[w, 1].astype(jnp.float32)
        top = (vis_real * first + vis_imag * second).astype(jnp.bfloat16)
        bottom = (vis_real * second - vis_imag * first).astype(jnp.bfloat16)
        rhs = jnp.concatenate(
            [jnp.concatenate([top, bottom], axis=1), jnp.concatenate([bottom, -top], axis=1)], axis=0
        )
        both = jnp.dot(u_ref[w], rhs, preferred_element_type=jnp.float32)
        out_ref[j, 0] = both[:, : 2 * S].astype(jnp.bfloat16)
        out_ref[j, 1] = both[:, 2 * S :].astype(jnp.bfloat16)


def patches_rotated(samples, planes, kernel_set):
    slots = samples.shape[0]
    u_kernel = jnp.transpose(kernel_set[:, :, :, :S], (0, 3, 1, 2)).reshape(NW, S, 2 * S)
    v_real = kernel_set[:, 0, :, S:]
    v_imag = kernel_set[:, 1, :, S:]
    v_parts = jnp.stack(
        [jnp.concatenate([v_real, v_imag], axis=-1), jnp.concatenate([-v_imag, v_real], axis=-1)], axis=1
    )
    grid_spec = pltpu.PrefetchScalarGridSpec(
        num_scalar_prefetch=1,
        grid=(slots // PATCH_CHUNK,),
        in_specs=[
            pl.BlockSpec((2 * S, PATCH_CHUNK), lambda i, p: (0, i)),
            pl.BlockSpec((NW, S, 2 * S), lambda i, p: (0, 0, 0)),
            pl.BlockSpec((NW, 2, S, 2 * S), lambda i, p: (0, 0, 0, 0)),
        ],
        out_specs=pl.BlockSpec((PATCH_CHUNK, 2, S, 2 * S), lambda i, p: (i, 0, 0, 0)),
    )
    return pl.pallas_call(
        patch_kernel,
        grid_spec=grid_spec,
        out_shape=jax.ShapeDtypeStruct((slots, 2, S, 2 * S), jnp.bfloat16),
        cost_estimate=pl.CostEstimate(
            flops=2 * slots * S * 2 * S * 4 * S, transcendentals=0, bytes_accessed=slots * 2 * S * 2 * S * 2 * 2
        ),
    )(planes, jnp.transpose(samples), u_kernel, v_parts)


def phase_index(rows, cols):
    spacing = G // P_SIZE - 1
    return jnp.mod(rows[:, None] * (spacing * cols[None, :]), G)


def cos_sin_f32(index):
    angle = index.astype(jnp.float32) * (2.0 * math.pi / G)
    return jnp.cos(angle), jnp.sin(angle)


def local(visibilities, kernels, destination, cell, plane):
    tile_count = lax.axis_size("tile")
    tile_index = lax.axis_index("tile")
    samples = visibilities[0]
    kernel_set = kernels[0]
    owners = destination[0, :, 0]
    blocks = samples.shape[0]
    capacity = 3 * blocks // tile_count
    spacing = G // P_SIZE - 1

    counts = jnp.sum(
        (owners[:, None] == jnp.arange(tile_count, dtype=jnp.int32)[None, :]).astype(jnp.int32), axis=0
    )
    first = jnp.cumsum(counts) - counts
    order = jnp.argsort(owners, stable=True).astype(jnp.int32)
    slot = jnp.arange(capacity, dtype=jnp.int32)
    valid = slot[None, :] < counts[:, None]
    src = order[jnp.clip(first[:, None] + slot[None, :], 0, blocks - 1)]
    packed_meta = cell[0] * NW + plane[0]
    send_samples = jnp.where(valid[:, :, None], samples[src], 0.0)
    send_meta = jnp.where(valid, packed_meta[src], 0).astype(jnp.float32)
    meta_row = jnp.pad(send_meta, ((0, 0), (0, samples.shape[1] - capacity)))[:, None, :]
    arrived = lax.all_to_all(
        jnp.concatenate([send_samples, meta_row], axis=1), "tile", split_axis=0, concat_axis=0, tiled=True
    )
    slot_total = tile_count * capacity
    arrived_meta = arrived[:, capacity, :capacity].astype(jnp.int32).reshape(slot_total)
    arrived = arrived[:, :capacity, :].reshape(slot_total, samples.shape[1])

    slab_rows = G // tile_count
    row_cells = slab_rows // S
    cell_cols = G // S
    q_len = G // NF
    q_cells = q_len // S
    j_len = P_SIZE // NF

    cell_r = arrived_meta // NW
    plane_r = arrived_meta % NW
    p2 = patches_rotated(arrived, plane_r, kernel_set).reshape(slot_total, 2, S * 2 * S)

    a_s = cell_r // cell_cols
    cc_s = cell_r % cell_cols
    p_s = cc_s // q_cells
    qc_s = cc_s % q_cells
    resid = jnp.arange(NF, dtype=jnp.int32)
    ph_index = jnp.mod(spacing * (p_s[:, None] - NF // 2) * resid[None, :], NF)
    ph_angle = ph_index.astype(jnp.float32) * (2.0 * math.pi / NF)
    phase = jnp.stack([jnp.cos(ph_angle), jnp.sin(ph_angle)], axis=-1)
    place = (a_s[:, None] == jnp.arange(row_cells, dtype=jnp.int32)[None, :])[:, :, None] & (
        qc_s[:, None] == jnp.arange(q_cells, dtype=jnp.int32)[None, :]
    )[:, None, :]
    l2 = (place.astype(jnp.float32)[None, :, :, :, None] * jnp.transpose(phase, (1, 0, 2))[:, :, None, None, :])
    l2 = jnp.transpose(l2, (0, 2, 3, 1, 4)).astype(jnp.bfloat16)
    folded = jnp.einsum("raqsk,skn->raqn", l2, p2, preferred_element_type=jnp.float32).astype(jnp.bfloat16)
    folded = folded.reshape(NF, row_cells, q_cells, S, 2 * S)

    j_index = resid[:, None] + NF * (jnp.arange(j_len, dtype=jnp.int32)[None, :] - j_len // 2)
    coarse = jnp.arange(q_cells, dtype=jnp.int32) * S
    fine = jnp.arange(S, dtype=jnp.int32)
    ca, sa = cos_sin_f32(jnp.mod(coarse[None, :, None] * (spacing * j_index[:, None, :]), G))
    cb, sb = cos_sin_f32(jnp.mod(fine[None, :, None] * (spacing * j_index[:, None, :]), G))
    ca = jnp.tile(ca, (1, 1, 2))[:, :, None, :]
    sa = jnp.tile(sa, (1, 1, 2))[:, :, None, :]
    cb = jnp.tile(cb, (1, 2, 2))[:, None, :, :]
    sb = jnp.tile(sb, (1, 2, 2))[:, None, :, :]
    c1 = (ca * cb - sa * sb).astype(jnp.bfloat16)
    s1 = (sa * cb + ca * sb).astype(jnp.bfloat16)
    ri_in = lax.broadcasted_iota(jnp.int32, (1, 1, 2 * S, 2 * j_len), 2) // S
    ri_out = lax.broadcasted_iota(jnp.int32, (1, 1, 2 * S, 2 * j_len), 3) // j_len
    w1 = jnp.where(ri_in == ri_out, c1, jnp.where(ri_in == 0, s1, -s1))
    transformed = jnp.einsum("raqxk,rqkn->raxn", folded, w1, preferred_element_type=jnp.float32)
    transformed = transformed.astype(jnp.bfloat16).reshape(NF, slab_rows, 2, j_len)

    l_index = jnp.arange(P_SIZE, dtype=jnp.int32) - P_SIZE // 2
    row_base = (tile_index * slab_rows - G // 2) + jnp.arange(row_cells, dtype=jnp.int32) * S
    ca, sa = cos_sin_f32(phase_index(row_base, l_index))
    cb, sb = cos_sin_f32(phase_index(fine, l_index))
    c2 = (ca[:, None, :] * cb[None, :, :] - sa[:, None, :] * sb[None, :, :]).astype(jnp.bfloat16)
    s2 = (sa[:, None, :] * cb[None, :, :] + ca[:, None, :] * sb[None, :, :]).astype(jnp.bfloat16)
    c2 = c2.reshape(slab_rows, P_SIZE)
    s2 = s2.reshape(slab_rows, P_SIZE)
    e2 = jnp.stack([c2, -s2])
    partial = jnp.einsum("iul,ruij->lrj", e2, transformed, preferred_element_type=jnp.float32)
    chan_count = lax.axis_size("chan")
    partial = partial.reshape(P_SIZE, NF, tile_count, j_len // tile_count)
    partial = jnp.transpose(partial, (2, 0, 1, 3))
    partial = lax.all_to_all(partial.astype(jnp.bfloat16), "tile", split_axis=0, concat_axis=0, tiled=True)
    partial = jnp.sum(partial.astype(jnp.float32), axis=0)
    partial = partial.reshape(chan_count, P_SIZE // chan_count, NF, j_len // tile_count)
    partial = lax.all_to_all(partial.astype(jnp.bfloat16), "chan", split_axis=0, concat_axis=0, tiled=True)
    partial = jnp.sum(partial.astype(jnp.float32), axis=0)
    out = jnp.transpose(partial, (0, 2, 1))
    return out.reshape(out.shape[0], -1) * (1.0 / G)


def solution(mesh):
    placed = (
        P("chan", "tile", None),
        P("chan", None, None, None, None),
        P("chan", "tile", None),
        P("chan", "tile"),
        P("chan", "tile"),
    )
    return jax.shard_map(
        local, mesh=mesh, in_specs=placed, out_specs=P("chan", "tile"), check_vma=False
    )
```

```python
import math

import jax
import jax.numpy as jnp
from jax import lax
from jax.sharding import PartitionSpec as P
from jax.experimental import pallas as pl
from jax.experimental.pallas import tpu as pltpu

G = 8192
S = 64
NW = 32
P_SIZE = 1024
NF = 8


def block_patches(samples, kernel_rows):
    sample_count = samples.shape[1] // 2
    support = kernel_rows.shape[3] // 2
    vis_real = samples[:, :sample_count, None]
    vis_imag = samples[:, sample_count:, None]
    kern_real = kernel_rows[:, 0].astype(jnp.float32)
    kern_imag = kernel_rows[:, 1].astype(jnp.float32)
    full_real = (vis_real * kern_real - vis_imag * kern_imag).astype(jnp.bfloat16)
    full_imag = (vis_real * kern_imag + vis_imag * kern_real).astype(jnp.bfloat16)
    weighted_real = full_real[:, :, support:]
    weighted_imag = full_imag[:, :, support:]
    v_weighted = jnp.stack(
        [
            jnp.concatenate([weighted_real, weighted_imag], axis=-1),
            jnp.concatenate([-weighted_imag, weighted_real], axis=-1),
        ],
        1,
    )
    patch = jnp.einsum("bpkx,bpkn->bxn", kernel_rows, v_weighted, preferred_element_type=jnp.float32)
    return patch[:, :support, :]


PATCH_CHUNK = 128


def patch_kernel(plane_ref, samples_ref, u_ref, v_ref, out_ref):
    base = pl.program_id(0) * PATCH_CHUNK
    for j in range(PATCH_CHUNK):
        w = plane_ref[base + j]
        column = samples_ref[:, j : j + 1]
        vis_real = column[:S]
        vis_imag = column[S:]
        first = v_ref[w, 0].astype(jnp.float32)
        second = v_ref[w, 1].astype(jnp.float32)
        top = (vis_real * first + vis_imag * second).astype(jnp.bfloat16)
        bottom = (vis_real * second - vis_imag * first).astype(jnp.bfloat16)
        rhs = jnp.concatenate(
            [jnp.concatenate([top, bottom], axis=1), jnp.concatenate([bottom, -top], axis=1)], axis=0
        )
        both = jnp.dot(u_ref[w], rhs, preferred_element_type=jnp.float32)
        out_ref[j, 0] = both[:, : 2 * S].astype(jnp.bfloat16)
        out_ref[j, 1] = both[:, 2 * S :].astype(jnp.bfloat16)


def patches_rotated(samples, planes, kernel_set):
    slots = samples.shape[0]
    u_kernel = jnp.transpose(kernel_set[:, :, :, :S], (0, 3, 1, 2)).reshape(NW, S, 2 * S)
    v_real = kernel_set[:, 0, :, S:]
    v_imag = kernel_set[:, 1, :, S:]
    v_parts = jnp.stack(
        [jnp.concatenate([v_real, v_imag], axis=-1), jnp.concatenate([-v_imag, v_real], axis=-1)], axis=1
    )
    grid_spec = pltpu.PrefetchScalarGridSpec(
        num_scalar_prefetch=1,
        grid=(slots // PATCH_CHUNK,),
        in_specs=[
            pl.BlockSpec((2 * S, PATCH_CHUNK), lambda i, p: (0, i)),
            pl.BlockSpec((NW, S, 2 * S), lambda i, p: (0, 0, 0)),
            pl.BlockSpec((NW, 2, S, 2 * S), lambda i, p: (0, 0, 0, 0)),
        ],
        out_specs=pl.BlockSpec((PATCH_CHUNK, 2, S, 2 * S), lambda i, p: (i, 0, 0, 0)),
    )
    return pl.pallas_call(
        patch_kernel,
        grid_spec=grid_spec,
        out_shape=jax.ShapeDtypeStruct((slots, 2, S, 2 * S), jnp.bfloat16),
        cost_estimate=pl.CostEstimate(
            flops=2 * slots * S * 2 * S * 4 * S, transcendentals=0, bytes_accessed=slots * 2 * S * 2 * S * 2 * 2
        ),
    )(planes, jnp.transpose(samples), u_kernel, v_parts)


def phase_index(rows, cols):
    spacing = G // P_SIZE - 1
    return jnp.mod(rows[:, None] * (spacing * cols[None, :]), G)


def cos_sin_f32(index):
    angle = index.astype(jnp.float32) * (2.0 * math.pi / G)
    return jnp.cos(angle), jnp.sin(angle)


def local(visibilities, kernels, destination, cell, plane):
    tile_count = lax.axis_size("tile")
    tile_index = lax.axis_index("tile")
    samples = visibilities[0]
    kernel_set = kernels[0]
    owners = destination[0, :, 0]
    blocks = samples.shape[0]
    capacity = 3 * blocks // tile_count
    spacing = G // P_SIZE - 1

    counts = jnp.sum(
        (owners[:, None] == jnp.arange(tile_count, dtype=jnp.int32)[None, :]).astype(jnp.int32), axis=0
    )
    first = jnp.cumsum(counts) - counts
    order = jnp.argsort(owners, stable=True).astype(jnp.int32)
    slot = jnp.arange(capacity, dtype=jnp.int32)
    valid = slot[None, :] < counts[:, None]
    src = order[jnp.clip(first[:, None] + slot[None, :], 0, blocks - 1)]
    packed_meta = cell[0] * NW + plane[0]
    send_samples = jnp.where(valid[:, :, None], samples[src], 0.0)
    send_meta = jnp.where(valid, packed_meta[src], 0).astype(jnp.float32)
    meta_row = jnp.pad(send_meta, ((0, 0), (0, samples.shape[1] - capacity)))[:, None, :]
    arrived = lax.all_to_all(
        jnp.concatenate([send_samples, meta_row], axis=1), "tile", split_axis=0, concat_axis=0, tiled=True
    )
    slot_total = tile_count * capacity
    arrived_meta = arrived[:, capacity, :capacity].astype(jnp.int32).reshape(slot_total)
    arrived = arrived[:, :capacity, :].reshape(slot_total, samples.shape[1])

    slab_rows = G // tile_count
    row_cells = slab_rows // S
    cell_cols = G // S
    q_len = G // NF
    q_cells = q_len // S
    j_len = P_SIZE // NF

    cell_r = arrived_meta // NW
    plane_r = arrived_meta % NW
    p2 = patches_rotated(arrived, plane_r, kernel_set).reshape(slot_total, 2, S * 2 * S)

    a_s = cell_r // cell_cols
    cc_s = cell_r % cell_cols
    p_s = cc_s // q_cells
    qc_s = cc_s % q_cells
    resid = jnp.arange(NF, dtype=jnp.int32)
    ph_index = jnp.mod(spacing * (p_s[:, None] - NF // 2) * resid[None, :], NF)
    ph_angle = ph_index.astype(jnp.float32) * (2.0 * math.pi / NF)
    phase = jnp.stack([jnp.cos(ph_angle), jnp.sin(ph_angle)], axis=-1)
    place = (a_s[:, None] == jnp.arange(row_cells, dtype=jnp.int32)[None, :])[:, :, None] & (
        qc_s[:, None] == jnp.arange(q_cells, dtype=jnp.int32)[None, :]
    )[:, None, :]
    l2 = (place.astype(jnp.float32)[None, :, :, :, None] * jnp.transpose(phase, (1, 0, 2))[:, :, None, None, :])
    l2 = jnp.transpose(l2, (0, 2, 3, 1, 4)).astype(jnp.bfloat16)
    j_index = resid[:, None] + NF * (jnp.arange(j_len, dtype=jnp.int32)[None, :] - j_len // 2)
    coarse = jnp.arange(q_cells, dtype=jnp.int32) * S
    fine = jnp.arange(S, dtype=jnp.int32)
    ca, sa = cos_sin_f32(jnp.mod(coarse[None, :, None] * (spacing * j_index[:, None, :]), G))
    cb, sb = cos_sin_f32(jnp.mod(fine[None, :, None] * (spacing * j_index[:, None, :]), G))
    ca = jnp.tile(ca, (1, 1, 2))[:, :, None, :]
    sa = jnp.tile(sa, (1, 1, 2))[:, :, None, :]
    cb = jnp.tile(cb, (1, 2, 2))[:, None, :, :]
    sb = jnp.tile(sb, (1, 2, 2))[:, None, :, :]
    c1 = (ca * cb - sa * sb).astype(jnp.bfloat16)
    s1 = (sa * cb + ca * sb).astype(jnp.bfloat16)
    ri_in = lax.broadcasted_iota(jnp.int32, (1, 1, 2 * S, 2 * j_len), 2) // S
    ri_out = lax.broadcasted_iota(jnp.int32, (1, 1, 2 * S, 2 * j_len), 3) // j_len
    w1 = jnp.where(ri_in == ri_out, c1, jnp.where(ri_in == 0, s1, -s1))
    l_index = jnp.arange(P_SIZE, dtype=jnp.int32) - P_SIZE // 2
    row_base = (tile_index * slab_rows - G // 2) + jnp.arange(row_cells, dtype=jnp.int32) * S
    ca, sa = cos_sin_f32(phase_index(row_base, l_index))
    cb, sb = cos_sin_f32(phase_index(fine, l_index))
    c2 = (ca[:, None, :] * cb[None, :, :] - sa[:, None, :] * sb[None, :, :]).astype(jnp.bfloat16)
    s2 = (sa[:, None, :] * cb[None, :, :] + ca[:, None, :] * sb[None, :, :]).astype(jnp.bfloat16)
    c2 = c2.reshape(slab_rows, P_SIZE)
    s2 = s2.reshape(slab_rows, P_SIZE)
    e2 = jnp.stack([c2, -s2])
    chan_count = lax.axis_size("chan")
    halves = 2
    per_half = NF // halves
    pieces = []
    for h in range(halves):
        rows = slice(h * per_half, (h + 1) * per_half)
        folded = jnp.einsum("raqsk,skn->raqn", l2[rows], p2, preferred_element_type=jnp.float32)
        folded = folded.astype(jnp.bfloat16).reshape(per_half, row_cells, q_cells, S, 2 * S)
        transformed = jnp.einsum("raqxk,rqkn->raxn", folded, w1[rows], preferred_element_type=jnp.float32)
        transformed = transformed.astype(jnp.bfloat16).reshape(per_half, slab_rows, 2, j_len)
        partial = jnp.einsum("iul,ruij->lrj", e2, transformed, preferred_element_type=jnp.float32)
        partial = partial.reshape(chan_count, P_SIZE // chan_count, per_half, j_len)
        partial = lax.all_to_all(partial.astype(jnp.bfloat16), "chan", split_axis=0, concat_axis=0, tiled=True)
        partial = jnp.sum(partial.astype(jnp.float32), axis=0)
        partial = partial.reshape(P_SIZE // chan_count, per_half, tile_count, j_len // tile_count)
        partial = jnp.transpose(partial, (2, 0, 1, 3))
        partial = lax.all_to_all(partial.astype(jnp.bfloat16), "tile", split_axis=0, concat_axis=0, tiled=True)
        pieces.append(jnp.sum(partial.astype(jnp.float32), axis=0))
    partial = jnp.concatenate(pieces, axis=1)
    out = jnp.transpose(partial, (0, 2, 1))
    return out.reshape(out.shape[0], -1) * (1.0 / G)


def solution(mesh):
    placed = (
        P("chan", "tile", None),
        P("chan", None, None, None, None),
        P("chan", "tile", None),
        P("chan", "tile"),
        P("chan", "tile"),
    )
    return jax.shard_map(
        local, mesh=mesh, in_specs=placed, out_specs=P("chan", "tile"), check_vma=False
    )
```

```python
import math

import jax
import jax.numpy as jnp
from jax import lax
from jax.sharding import PartitionSpec as P
from jax.experimental import pallas as pl
from jax.experimental.pallas import tpu as pltpu

G = 8192
S = 64
NW = 32
P_SIZE = 1024
NF = 8


def block_patches(samples, kernel_rows):
    sample_count = samples.shape[1] // 2
    support = kernel_rows.shape[3] // 2
    vis_real = samples[:, :sample_count, None]
    vis_imag = samples[:, sample_count:, None]
    kern_real = kernel_rows[:, 0].astype(jnp.float32)
    kern_imag = kernel_rows[:, 1].astype(jnp.float32)
    full_real = (vis_real * kern_real - vis_imag * kern_imag).astype(jnp.bfloat16)
    full_imag = (vis_real * kern_imag + vis_imag * kern_real).astype(jnp.bfloat16)
    weighted_real = full_real[:, :, support:]
    weighted_imag = full_imag[:, :, support:]
    v_weighted = jnp.stack(
        [
            jnp.concatenate([weighted_real, weighted_imag], axis=-1),
            jnp.concatenate([-weighted_imag, weighted_real], axis=-1),
        ],
        1,
    )
    patch = jnp.einsum("bpkx,bpkn->bxn", kernel_rows, v_weighted, preferred_element_type=jnp.float32)
    return patch[:, :support, :]


PATCH_CHUNK = 128


def patch_kernel(plane_ref, samples_ref, u_ref, v_ref, out_ref):
    base = pl.program_id(0) * PATCH_CHUNK
    for j in range(PATCH_CHUNK):
        w = plane_ref[base + j]
        column = samples_ref[:, j : j + 1]
        vis_real = column[:S]
        vis_imag = column[S:]
        first = v_ref[w, 0].astype(jnp.float32)
        second = v_ref[w, 1].astype(jnp.float32)
        top = (vis_real * first + vis_imag * second).astype(jnp.bfloat16)
        bottom = (vis_real * second - vis_imag * first).astype(jnp.bfloat16)
        rhs = jnp.concatenate(
            [jnp.concatenate([top, bottom], axis=1), jnp.concatenate([bottom, -top], axis=1)], axis=0
        )
        both = jnp.dot(u_ref[w], rhs, preferred_element_type=jnp.float32)
        out_ref[j, 0] = both[:, : 2 * S].astype(jnp.bfloat16)
        out_ref[j, 1] = both[:, 2 * S :].astype(jnp.bfloat16)


def patches_rotated(samples, planes, kernel_set):
    slots = samples.shape[0]
    u_kernel = jnp.transpose(kernel_set[:, :, :, :S], (0, 3, 1, 2)).reshape(NW, S, 2 * S)
    v_real = kernel_set[:, 0, :, S:]
    v_imag = kernel_set[:, 1, :, S:]
    v_parts = jnp.stack(
        [jnp.concatenate([v_real, v_imag], axis=-1), jnp.concatenate([-v_imag, v_real], axis=-1)], axis=1
    )
    grid_spec = pltpu.PrefetchScalarGridSpec(
        num_scalar_prefetch=1,
        grid=(slots // PATCH_CHUNK,),
        in_specs=[
            pl.BlockSpec((2 * S, PATCH_CHUNK), lambda i, p: (0, i)),
            pl.BlockSpec((NW, S, 2 * S), lambda i, p: (0, 0, 0)),
            pl.BlockSpec((NW, 2, S, 2 * S), lambda i, p: (0, 0, 0, 0)),
        ],
        out_specs=pl.BlockSpec((PATCH_CHUNK, 2, S, 2 * S), lambda i, p: (i, 0, 0, 0)),
    )
    return pl.pallas_call(
        patch_kernel,
        grid_spec=grid_spec,
        out_shape=jax.ShapeDtypeStruct((slots, 2, S, 2 * S), jnp.bfloat16),
        cost_estimate=pl.CostEstimate(
            flops=2 * slots * S * 2 * S * 4 * S, transcendentals=0, bytes_accessed=slots * 2 * S * 2 * S * 2 * 2
        ),
    )(planes, jnp.transpose(samples), u_kernel, v_parts)


def phase_index(rows, cols):
    spacing = G // P_SIZE - 1
    return jnp.mod(rows[:, None] * (spacing * cols[None, :]), G)


def cos_sin_f32(index):
    angle = index.astype(jnp.float32) * (2.0 * math.pi / G)
    return jnp.cos(angle), jnp.sin(angle)


def local(visibilities, kernels, destination, cell, plane):
    tile_count = lax.axis_size("tile")
    tile_index = lax.axis_index("tile")
    samples = visibilities[0]
    kernel_set = kernels[0]
    owners = destination[0, :, 0]
    blocks = samples.shape[0]
    capacity = 3 * blocks // tile_count
    spacing = G // P_SIZE - 1

    tiles = jnp.arange(tile_count, dtype=jnp.int32)
    onehot = (owners[:, None] == tiles[None, :]).astype(jnp.int32)
    rank = jnp.sum(jnp.cumsum(onehot, axis=0) * onehot, axis=1) - 1
    slot = jnp.arange(capacity, dtype=jnp.int32)
    pick = (owners[None, None, :] == tiles[:, None, None]) & (rank[None, None, :] == slot[None, :, None])
    pick = pick.astype(jnp.float32).reshape(tile_count * capacity, blocks)
    packed_meta = (cell[0] * NW + plane[0]).astype(jnp.float32)
    routed = jnp.dot(
        pick, jnp.concatenate([samples, packed_meta[:, None]], axis=1), precision=lax.Precision.HIGHEST
    )
    send_samples = routed[:, : samples.shape[1]].reshape(tile_count, capacity, samples.shape[1])
    send_meta = routed[:, samples.shape[1]].reshape(tile_count, capacity)
    meta_row = jnp.pad(send_meta, ((0, 0), (0, samples.shape[1] - capacity)))[:, None, :]
    arrived = lax.all_to_all(
        jnp.concatenate([send_samples, meta_row], axis=1), "tile", split_axis=0, concat_axis=0, tiled=True
    )
    slot_total = tile_count * capacity
    arrived_meta = arrived[:, capacity, :capacity].astype(jnp.int32).reshape(slot_total)
    arrived = arrived[:, :capacity, :].reshape(slot_total, samples.shape[1])

    slab_rows = G // tile_count
    row_cells = slab_rows // S
    cell_cols = G // S
    q_len = G // NF
    q_cells = q_len // S
    j_len = P_SIZE // NF

    cell_r = arrived_meta // NW
    plane_r = arrived_meta % NW
    p2 = patches_rotated(arrived, plane_r, kernel_set).reshape(slot_total, 2, S * 2 * S)

    a_s = cell_r // cell_cols
    cc_s = cell_r % cell_cols
    p_s = cc_s // q_cells
    qc_s = cc_s % q_cells
    resid = jnp.arange(NF, dtype=jnp.int32)
    ph_index = jnp.mod(spacing * (p_s[:, None] - NF // 2) * resid[None, :], NF)
    ph_angle = ph_index.astype(jnp.float32) * (2.0 * math.pi / NF)
    phase = jnp.stack([jnp.cos(ph_angle), jnp.sin(ph_angle)], axis=-1)
    place = (a_s[:, None] == jnp.arange(row_cells, dtype=jnp.int32)[None, :])[:, :, None] & (
        qc_s[:, None] == jnp.arange(q_cells, dtype=jnp.int32)[None, :]
    )[:, None, :]
    l2 = (place.astype(jnp.float32)[None, :, :, :, None] * jnp.transpose(phase, (1, 0, 2))[:, :, None, None, :])
    l2 = jnp.transpose(l2, (0, 2, 3, 1, 4)).astype(jnp.bfloat16)
    folded = jnp.einsum("raqsk,skn->raqn", l2, p2, preferred_element_type=jnp.float32).astype(jnp.bfloat16)
    folded = folded.reshape(NF, row_cells, q_cells, S, 2 * S)

    coarse = jnp.arange(q_cells, dtype=jnp.int32) * S
    fine = jnp.arange(S, dtype=jnp.int32)
    n_full = jnp.arange(2 * j_len, dtype=jnp.int32) % j_len
    j_full = resid[:, None] + NF * (n_full[None, :] - j_len // 2)
    y_full = jnp.arange(2 * S, dtype=jnp.int32) % S
    ca, sa = cos_sin_f32(jnp.mod(coarse[None, :, None] * (spacing * j_full[:, None, :]), G))
    cb, sb = cos_sin_f32(jnp.mod(y_full[None, :, None] * (spacing * j_full[:, None, :]), G))
    ca = ca[:, :, None, :]
    sa = sa[:, :, None, :]
    cb = cb[:, None, :, :]
    sb = sb[:, None, :, :]
    c1 = (ca * cb - sa * sb).astype(jnp.bfloat16)
    s1 = (sa * cb + ca * sb).astype(jnp.bfloat16)
    ri_in = lax.broadcasted_iota(jnp.int32, (1, 1, 2 * S, 2 * j_len), 2) // S
    ri_out = lax.broadcasted_iota(jnp.int32, (1, 1, 2 * S, 2 * j_len), 3) // j_len
    w1 = jnp.where(ri_in == ri_out, c1, jnp.where(ri_in == 0, s1, -s1))
    transformed = jnp.einsum("raqxk,rqkn->raxn", folded, w1, preferred_element_type=jnp.float32)
    transformed = transformed.astype(jnp.bfloat16).reshape(NF, slab_rows, 2, j_len)

    l_index = jnp.arange(P_SIZE, dtype=jnp.int32) - P_SIZE // 2
    row_base = (tile_index * slab_rows - G // 2) + jnp.arange(row_cells, dtype=jnp.int32) * S
    ca, sa = cos_sin_f32(phase_index(l_index, row_base))
    cb, sb = cos_sin_f32(phase_index(l_index, fine))
    c2 = (ca[:, :, None] * cb[:, None, :] - sa[:, :, None] * sb[:, None, :]).astype(jnp.bfloat16)
    s2 = (sa[:, :, None] * cb[:, None, :] + ca[:, :, None] * sb[:, None, :]).astype(jnp.bfloat16)
    c2 = c2.reshape(P_SIZE, slab_rows)
    s2 = s2.reshape(P_SIZE, slab_rows)
    e2 = jnp.stack([c2, -s2], axis=1)
    partial = jnp.einsum("liu,ruij->lrj", e2, transformed, preferred_element_type=jnp.float32)
    chan_count = lax.axis_size("chan")
    partial = partial.reshape(chan_count, P_SIZE // chan_count, NF, j_len)
    partial = lax.all_to_all(partial.astype(jnp.bfloat16), "chan", split_axis=0, concat_axis=0, tiled=True)
    partial = jnp.sum(partial.astype(jnp.float32), axis=0)
    partial = partial.reshape(P_SIZE // chan_count, NF, tile_count, j_len // tile_count)
    partial = jnp.transpose(partial, (2, 0, 1, 3))
    partial = lax.all_to_all(partial.astype(jnp.bfloat16), "tile", split_axis=0, concat_axis=0, tiled=True)
    partial = jnp.sum(partial.astype(jnp.float32), axis=0)
    out = jnp.transpose(partial, (0, 2, 1))
    return out.reshape(out.shape[0], -1) * (1.0 / G)


def solution(mesh):
    placed = (
        P("chan", "tile", None),
        P("chan", None, None, None, None),
        P("chan", "tile", None),
        P("chan", "tile"),
        P("chan", "tile"),
    )
    return jax.shard_map(
        local, mesh=mesh, in_specs=placed, out_specs=P("chan", "tile"), check_vma=False
    )
```

```python
import math

import jax
import jax.numpy as jnp
from jax import lax
from jax.sharding import PartitionSpec as P
from jax.experimental import pallas as pl
from jax.experimental.pallas import tpu as pltpu

G = 8192
S = 64
NW = 32
P_SIZE = 1024
NF = 8


def block_patches(samples, kernel_rows):
    sample_count = samples.shape[1] // 2
    support = kernel_rows.shape[3] // 2
    vis_real = samples[:, :sample_count, None]
    vis_imag = samples[:, sample_count:, None]
    kern_real = kernel_rows[:, 0].astype(jnp.float32)
    kern_imag = kernel_rows[:, 1].astype(jnp.float32)
    full_real = (vis_real * kern_real - vis_imag * kern_imag).astype(jnp.bfloat16)
    full_imag = (vis_real * kern_imag + vis_imag * kern_real).astype(jnp.bfloat16)
    weighted_real = full_real[:, :, support:]
    weighted_imag = full_imag[:, :, support:]
    v_weighted = jnp.stack(
        [
            jnp.concatenate([weighted_real, weighted_imag], axis=-1),
            jnp.concatenate([-weighted_imag, weighted_real], axis=-1),
        ],
        1,
    )
    patch = jnp.einsum("bpkx,bpkn->bxn", kernel_rows, v_weighted, preferred_element_type=jnp.float32)
    return patch[:, :support, :]


PATCH_CHUNK = 128


def patch_kernel(plane_ref, samples_ref, u_ref, v_ref, out_ref):
    base = pl.program_id(0) * PATCH_CHUNK
    for j in range(PATCH_CHUNK):
        w = plane_ref[base + j]
        column = samples_ref[:, j : j + 1]
        vis_real = column[:S]
        vis_imag = column[S:]
        first = v_ref[w, 0].astype(jnp.float32)
        second = v_ref[w, 1].astype(jnp.float32)
        top = (vis_real * first + vis_imag * second).astype(jnp.bfloat16)
        bottom = (vis_real * second - vis_imag * first).astype(jnp.bfloat16)
        rhs = jnp.concatenate(
            [jnp.concatenate([top, bottom], axis=1), jnp.concatenate([bottom, -top], axis=1)], axis=0
        )
        both = jnp.dot(u_ref[w], rhs, preferred_element_type=jnp.float32)
        out_ref[j, 0] = both[:, : 2 * S].astype(jnp.bfloat16)
        out_ref[j, 1] = both[:, 2 * S :].astype(jnp.bfloat16)


def patches_rotated(samples, planes, kernel_set):
    slots = samples.shape[0]
    u_kernel = jnp.transpose(kernel_set[:, :, :, :S], (0, 3, 1, 2)).reshape(NW, S, 2 * S)
    v_real = kernel_set[:, 0, :, S:]
    v_imag = kernel_set[:, 1, :, S:]
    v_parts = jnp.stack(
        [jnp.concatenate([v_real, v_imag], axis=-1), jnp.concatenate([-v_imag, v_real], axis=-1)], axis=1
    )
    grid_spec = pltpu.PrefetchScalarGridSpec(
        num_scalar_prefetch=1,
        grid=(slots // PATCH_CHUNK,),
        in_specs=[
            pl.BlockSpec((2 * S, PATCH_CHUNK), lambda i, p: (0, i)),
            pl.BlockSpec((NW, S, 2 * S), lambda i, p: (0, 0, 0)),
            pl.BlockSpec((NW, 2, S, 2 * S), lambda i, p: (0, 0, 0, 0)),
        ],
        out_specs=pl.BlockSpec((PATCH_CHUNK, 2, S, 2 * S), lambda i, p: (i, 0, 0, 0)),
    )
    return pl.pallas_call(
        patch_kernel,
        grid_spec=grid_spec,
        out_shape=jax.ShapeDtypeStruct((slots, 2, S, 2 * S), jnp.bfloat16),
        cost_estimate=pl.CostEstimate(
            flops=2 * slots * S * 2 * S * 4 * S, transcendentals=0, bytes_accessed=slots * 2 * S * 2 * S * 2 * 2
        ),
    )(planes, jnp.transpose(samples), u_kernel, v_parts)


def phase_index(rows, cols):
    spacing = G // P_SIZE - 1
    return jnp.mod(rows[:, None] * (spacing * cols[None, :]), G)


def cos_sin_f32(index):
    angle = index.astype(jnp.float32) * (2.0 * math.pi / G)
    return jnp.cos(angle), jnp.sin(angle)


def local(visibilities, kernels, destination, cell, plane):
    tile_count = lax.axis_size("tile")
    tile_index = lax.axis_index("tile")
    samples = visibilities[0]
    kernel_set = kernels[0]
    owners = destination[0, :, 0]
    blocks = samples.shape[0]
    capacity = 3 * blocks // tile_count
    spacing = G // P_SIZE - 1

    tiles = jnp.arange(tile_count, dtype=jnp.int32)
    onehot = (owners[:, None] == tiles[None, :]).astype(jnp.int32)
    rank = jnp.sum(jnp.cumsum(onehot, axis=0) * onehot, axis=1) - 1
    slot = jnp.arange(capacity, dtype=jnp.int32)
    pick = (owners[None, None, :] == tiles[:, None, None]) & (rank[None, None, :] == slot[None, :, None])
    pick = pick.astype(jnp.float32).reshape(tile_count * capacity, blocks)
    packed_meta = (cell[0] * NW + plane[0]).astype(jnp.float32)
    routed = jnp.dot(
        pick, jnp.concatenate([samples, packed_meta[:, None]], axis=1), precision=lax.Precision.HIGHEST
    )
    send_samples = routed[:, : samples.shape[1]].reshape(tile_count, capacity, samples.shape[1])
    send_meta = routed[:, samples.shape[1]].reshape(tile_count, capacity)
    meta_row = jnp.pad(send_meta, ((0, 0), (0, samples.shape[1] - capacity)))[:, None, :]
    arrived = lax.all_to_all(
        jnp.concatenate([send_samples, meta_row], axis=1), "tile", split_axis=0, concat_axis=0, tiled=True
    )
    slot_total = tile_count * capacity
    arrived_meta = arrived[:, capacity, :capacity].astype(jnp.int32).reshape(slot_total)
    arrived = arrived[:, :capacity, :].reshape(slot_total, samples.shape[1])

    slab_rows = G // tile_count
    row_cells = slab_rows // S
    cell_cols = G // S
    q_len = G // NF
    q_cells = q_len // S
    j_len = P_SIZE // NF

    cell_r = arrived_meta // NW
    plane_r = arrived_meta % NW
    p2 = patches_rotated(arrived, plane_r, kernel_set).reshape(slot_total * 2, S * 2 * S)

    a_s = cell_r // cell_cols
    cc_s = cell_r % cell_cols
    p_s = cc_s // q_cells
    qc_s = cc_s % q_cells
    resid = jnp.arange(NF, dtype=jnp.int32)
    ph_index = jnp.mod(spacing * (p_s[:, None] - NF // 2) * resid[None, :], NF)
    ph_angle = ph_index.astype(jnp.float32) * (2.0 * math.pi / NF)
    phase = jnp.stack([jnp.cos(ph_angle), jnp.sin(ph_angle)], axis=-1)
    place = (a_s[:, None] == jnp.arange(row_cells, dtype=jnp.int32)[None, :])[:, :, None] & (
        qc_s[:, None] == jnp.arange(q_cells, dtype=jnp.int32)[None, :]
    )[:, None, :]
    l2 = (place.astype(jnp.float32)[None, :, :, :, None] * jnp.transpose(phase, (1, 0, 2))[:, :, None, None, :])
    l2 = jnp.transpose(l2, (0, 2, 3, 1, 4)).astype(jnp.bfloat16)
    l2 = l2.reshape(NF * row_cells * q_cells, slot_total * 2)
    folded = jnp.dot(l2, p2, preferred_element_type=jnp.float32).astype(jnp.bfloat16)
    folded = folded.reshape(NF, row_cells, q_cells, S, 2 * S)

    coarse = jnp.arange(q_cells, dtype=jnp.int32) * S
    fine = jnp.arange(S, dtype=jnp.int32)
    n_full = jnp.arange(2 * j_len, dtype=jnp.int32) % j_len
    j_full = resid[:, None] + NF * (n_full[None, :] - j_len // 2)
    y_full = jnp.arange(2 * S, dtype=jnp.int32) % S
    ca, sa = cos_sin_f32(jnp.mod(coarse[None, :, None] * (spacing * j_full[:, None, :]), G))
    cb, sb = cos_sin_f32(jnp.mod(y_full[None, :, None] * (spacing * j_full[:, None, :]), G))
    ca = ca[:, :, None, :]
    sa = sa[:, :, None, :]
    cb = cb[:, None, :, :]
    sb = sb[:, None, :, :]
    c1 = (ca * cb - sa * sb).astype(jnp.bfloat16)
    s1 = (sa * cb + ca * sb).astype(jnp.bfloat16)
    ri_in = lax.broadcasted_iota(jnp.int32, (1, 1, 2 * S, 2 * j_len), 2) // S
    ri_out = lax.broadcasted_iota(jnp.int32, (1, 1, 2 * S, 2 * j_len), 3) // j_len
    w1 = jnp.where(ri_in == ri_out, c1, jnp.where(ri_in == 0, s1, -s1))
    transformed = jnp.einsum("raqxk,rqkn->raxn", folded, w1, preferred_element_type=jnp.float32)
    transformed = transformed.astype(jnp.bfloat16).reshape(NF, slab_rows, 2, j_len)

    l_index = jnp.arange(P_SIZE, dtype=jnp.int32) - P_SIZE // 2
    row_base = (tile_index * slab_rows - G // 2) + jnp.arange(row_cells, dtype=jnp.int32) * S
    ca, sa = cos_sin_f32(phase_index(l_index, row_base))
    cb, sb = cos_sin_f32(phase_index(l_index, fine))
    c2 = (ca[:, :, None] * cb[:, None, :] - sa[:, :, None] * sb[:, None, :]).astype(jnp.bfloat16)
    s2 = (sa[:, :, None] * cb[:, None, :] + ca[:, :, None] * sb[:, None, :]).astype(jnp.bfloat16)
    c2 = c2.reshape(P_SIZE, slab_rows)
    s2 = s2.reshape(P_SIZE, slab_rows)
    e2 = jnp.stack([c2, -s2], axis=1)
    partial = jnp.einsum("liu,ruij->lrj", e2, transformed, preferred_element_type=jnp.float32)
    chan_count = lax.axis_size("chan")
    partial = partial.reshape(chan_count, P_SIZE // chan_count, NF, j_len)
    partial = lax.all_to_all(partial.astype(jnp.bfloat16), "chan", split_axis=0, concat_axis=0, tiled=True)
    partial = jnp.sum(partial.astype(jnp.float32), axis=0)
    partial = partial.reshape(P_SIZE // chan_count, NF, tile_count, j_len // tile_count)
    partial = jnp.transpose(partial, (2, 0, 1, 3))
    partial = lax.all_to_all(partial.astype(jnp.bfloat16), "tile", split_axis=0, concat_axis=0, tiled=True)
    partial = jnp.sum(partial.astype(jnp.float32), axis=0)
    out = jnp.transpose(partial, (0, 2, 1))
    return out.reshape(out.shape[0], -1) * (1.0 / G)


def solution(mesh):
    placed = (
        P("chan", "tile", None),
        P("chan", None, None, None, None),
        P("chan", "tile", None),
        P("chan", "tile"),
        P("chan", "tile"),
    )
    return jax.shard_map(
        local, mesh=mesh, in_specs=placed, out_specs=P("chan", "tile"), check_vma=False
    )
```

```python
import math

import jax
import jax.numpy as jnp
from jax import lax
from jax.sharding import PartitionSpec as P
from jax.experimental import pallas as pl
from jax.experimental.pallas import tpu as pltpu

G = 8192
S = 64
NW = 32
P_SIZE = 1024
NF = 8


def block_patches(samples, kernel_rows):
    sample_count = samples.shape[1] // 2
    support = kernel_rows.shape[3] // 2
    vis_real = samples[:, :sample_count, None]
    vis_imag = samples[:, sample_count:, None]
    kern_real = kernel_rows[:, 0].astype(jnp.float32)
    kern_imag = kernel_rows[:, 1].astype(jnp.float32)
    full_real = (vis_real * kern_real - vis_imag * kern_imag).astype(jnp.bfloat16)
    full_imag = (vis_real * kern_imag + vis_imag * kern_real).astype(jnp.bfloat16)
    weighted_real = full_real[:, :, support:]
    weighted_imag = full_imag[:, :, support:]
    v_weighted = jnp.stack(
        [
            jnp.concatenate([weighted_real, weighted_imag], axis=-1),
            jnp.concatenate([-weighted_imag, weighted_real], axis=-1),
        ],
        1,
    )
    patch = jnp.einsum("bpkx,bpkn->bxn", kernel_rows, v_weighted, preferred_element_type=jnp.float32)
    return patch[:, :support, :]


PATCH_CHUNK = 128


def patch_kernel(plane_ref, samples_ref, u_ref, v_ref, out_ref):
    base = pl.program_id(0) * PATCH_CHUNK
    for j in range(PATCH_CHUNK):
        w = plane_ref[base + j]
        column = samples_ref[:, j : j + 1]
        vis_real = column[:S]
        vis_imag = column[S:]
        first = v_ref[w, 0].astype(jnp.float32)
        second = v_ref[w, 1].astype(jnp.float32)
        top = (vis_real * first + vis_imag * second).astype(jnp.bfloat16)
        bottom = (vis_real * second - vis_imag * first).astype(jnp.bfloat16)
        rhs = jnp.concatenate(
            [jnp.concatenate([top, bottom], axis=1), jnp.concatenate([bottom, -top], axis=1)], axis=0
        )
        both = jnp.dot(u_ref[w], rhs, preferred_element_type=jnp.float32)
        out_ref[j, 0] = both[:, : 2 * S].astype(jnp.bfloat16)
        out_ref[j, 1] = both[:, 2 * S :].astype(jnp.bfloat16)


def patches_rotated(samples, planes, kernel_set):
    slots = samples.shape[0]
    u_kernel = jnp.transpose(kernel_set[:, :, :, :S], (0, 3, 1, 2)).reshape(NW, S, 2 * S)
    v_real = kernel_set[:, 0, :, S:]
    v_imag = kernel_set[:, 1, :, S:]
    v_parts = jnp.stack(
        [jnp.concatenate([v_real, v_imag], axis=-1), jnp.concatenate([-v_imag, v_real], axis=-1)], axis=1
    )
    grid_spec = pltpu.PrefetchScalarGridSpec(
        num_scalar_prefetch=1,
        grid=(slots // PATCH_CHUNK,),
        in_specs=[
            pl.BlockSpec((2 * S, PATCH_CHUNK), lambda i, p: (0, i)),
            pl.BlockSpec((NW, S, 2 * S), lambda i, p: (0, 0, 0)),
            pl.BlockSpec((NW, 2, S, 2 * S), lambda i, p: (0, 0, 0, 0)),
        ],
        out_specs=pl.BlockSpec((PATCH_CHUNK, 2, S, 2 * S), lambda i, p: (i, 0, 0, 0)),
    )
    return pl.pallas_call(
        patch_kernel,
        grid_spec=grid_spec,
        out_shape=jax.ShapeDtypeStruct((slots, 2, S, 2 * S), jnp.bfloat16),
        cost_estimate=pl.CostEstimate(
            flops=2 * slots * S * 2 * S * 4 * S, transcendentals=0, bytes_accessed=slots * 2 * S * 2 * S * 2 * 2
        ),
    )(planes, jnp.transpose(samples), u_kernel, v_parts)


def phase_index(rows, cols):
    spacing = G // P_SIZE - 1
    return jnp.mod(rows[:, None] * (spacing * cols[None, :]), G)


def cos_sin_f32(index):
    angle = index.astype(jnp.float32) * (2.0 * math.pi / G)
    return jnp.cos(angle), jnp.sin(angle)


def local(visibilities, kernels, destination, cell, plane):
    tile_count = lax.axis_size("tile")
    tile_index = lax.axis_index("tile")
    samples = visibilities[0]
    kernel_set = kernels[0]
    owners = destination[0, :, 0]
    blocks = samples.shape[0]
    capacity = 3 * blocks // tile_count
    spacing = G // P_SIZE - 1

    tiles = jnp.arange(tile_count, dtype=jnp.int32)
    onehot = (owners[:, None] == tiles[None, :]).astype(jnp.int32)
    rank = jnp.sum(jnp.cumsum(onehot, axis=0) * onehot, axis=1) - 1
    slot = jnp.arange(capacity, dtype=jnp.int32)
    pick = (owners[None, None, :] == tiles[:, None, None]) & (rank[None, None, :] == slot[None, :, None])
    pick = pick.astype(jnp.float32).reshape(tile_count * capacity, blocks)
    packed_meta = (cell[0] * NW + plane[0]).astype(jnp.float32)
    routed = jnp.dot(
        pick, jnp.concatenate([samples, packed_meta[:, None]], axis=1), precision=lax.Precision.HIGHEST
    )
    send_samples = routed[:, : samples.shape[1]].reshape(tile_count, capacity, samples.shape[1])
    send_meta = routed[:, samples.shape[1]].reshape(tile_count, capacity)
    meta_row = jnp.pad(send_meta, ((0, 0), (0, samples.shape[1] - capacity)))[:, None, :]
    arrived = lax.all_to_all(
        jnp.concatenate([send_samples, meta_row], axis=1), "tile", split_axis=0, concat_axis=0, tiled=True
    )
    slot_total = tile_count * capacity
    arrived_meta = arrived[:, capacity, :capacity].astype(jnp.int32).reshape(slot_total)
    arrived = arrived[:, :capacity, :].reshape(slot_total, samples.shape[1])

    slab_rows = G // tile_count
    row_cells = slab_rows // S
    cell_cols = G // S
    q_len = G // NF
    q_cells = q_len // S
    j_len = P_SIZE // NF

    cell_r = arrived_meta // NW
    plane_r = arrived_meta % NW
    p2 = patches_rotated(arrived, plane_r, kernel_set).reshape(slot_total * 2, S * 2 * S)

    a_s = cell_r // cell_cols
    cc_s = cell_r % cell_cols
    p_s = cc_s // q_cells
    qc_s = cc_s % q_cells
    resid = jnp.arange(NF, dtype=jnp.int32)
    shape2 = (NF * row_cells * q_cells, slot_total * 2)
    row_id = lax.broadcasted_iota(jnp.int32, shape2, 0)
    col_id = lax.broadcasted_iota(jnp.int32, shape2, 1)
    r_m = row_id // (row_cells * q_cells)
    a_m = (row_id // q_cells) % row_cells
    q_m = row_id % q_cells
    a_c = jnp.repeat(a_s, 2)[None, :]
    qc_c = jnp.repeat(qc_s, 2)[None, :]
    p_c = jnp.repeat(p_s, 2)[None, :]
    ph_index = jnp.mod(spacing * (p_c - NF // 2) * r_m, NF)
    half = math.sqrt(0.5)
    cos_v = jnp.where(
        ph_index == 0,
        1.0,
        jnp.where(
            ph_index == 4,
            -1.0,
            jnp.where((ph_index == 2) | (ph_index == 6), 0.0, jnp.where((ph_index == 1) | (ph_index == 7), half, -half)),
        ),
    )
    sin_v = jnp.where(
        (ph_index == 0) | (ph_index == 4),
        0.0,
        jnp.where(
            ph_index == 2,
            1.0,
            jnp.where(ph_index == 6, -1.0, jnp.where((ph_index == 1) | (ph_index == 3), half, -half)),
        ),
    )
    inside = (a_c == a_m) & (qc_c == q_m)
    l2 = jnp.where(inside, jnp.where(col_id % 2 == 0, cos_v, sin_v), 0.0).astype(jnp.bfloat16)
    folded = jnp.dot(l2, p2, preferred_element_type=jnp.float32).astype(jnp.bfloat16)
    folded = folded.reshape(NF, row_cells, q_cells, S, 2 * S)

    coarse = jnp.arange(q_cells, dtype=jnp.int32) * S
    fine = jnp.arange(S, dtype=jnp.int32)
    n_full = jnp.arange(2 * j_len, dtype=jnp.int32) % j_len
    j_full = resid[:, None] + NF * (n_full[None, :] - j_len // 2)
    y_full = jnp.arange(2 * S, dtype=jnp.int32) % S
    ca, sa = cos_sin_f32(jnp.mod(coarse[None, :, None] * (spacing * j_full[:, None, :]), G))
    cb, sb = cos_sin_f32(jnp.mod(y_full[None, :, None] * (spacing * j_full[:, None, :]), G))
    ca = ca[:, :, None, :]
    sa = sa[:, :, None, :]
    cb = cb[:, None, :, :]
    sb = sb[:, None, :, :]
    c1 = (ca * cb - sa * sb).astype(jnp.bfloat16)
    s1 = (sa * cb + ca * sb).astype(jnp.bfloat16)
    ri_in = lax.broadcasted_iota(jnp.int32, (1, 1, 2 * S, 2 * j_len), 2) // S
    ri_out = lax.broadcasted_iota(jnp.int32, (1, 1, 2 * S, 2 * j_len), 3) // j_len
    w1 = jnp.where(ri_in == ri_out, c1, jnp.where(ri_in == 0, s1, -s1))
    transformed = jnp.einsum("raqxk,rqkn->raxn", folded, w1, preferred_element_type=jnp.float32)
    transformed = transformed.astype(jnp.bfloat16).reshape(NF, slab_rows, 2, j_len)

    l_index = jnp.arange(P_SIZE, dtype=jnp.int32) - P_SIZE // 2
    row_base = (tile_index * slab_rows - G // 2) + jnp.arange(row_cells, dtype=jnp.int32) * S
    ca, sa = cos_sin_f32(phase_index(l_index, row_base))
    cb, sb = cos_sin_f32(phase_index(l_index, fine))
    c2 = (ca[:, :, None] * cb[:, None, :] - sa[:, :, None] * sb[:, None, :]).astype(jnp.bfloat16)
    s2 = (sa[:, :, None] * cb[:, None, :] + ca[:, :, None] * sb[:, None, :]).astype(jnp.bfloat16)
    c2 = c2.reshape(P_SIZE, slab_rows)
    s2 = s2.reshape(P_SIZE, slab_rows)
    e2 = jnp.stack([c2, -s2], axis=1)
    partial = jnp.einsum("liu,ruij->lrj", e2, transformed, preferred_element_type=jnp.float32)
    chan_count = lax.axis_size("chan")
    partial = partial.reshape(chan_count, P_SIZE // chan_count, NF, j_len)
    partial = lax.all_to_all(partial.astype(jnp.bfloat16), "chan", split_axis=0, concat_axis=0, tiled=True)
    partial = jnp.sum(partial.astype(jnp.float32), axis=0)
    partial = partial.reshape(P_SIZE // chan_count, NF, tile_count, j_len // tile_count)
    partial = jnp.transpose(partial, (2, 0, 1, 3))
    partial = lax.all_to_all(partial.astype(jnp.bfloat16), "tile", split_axis=0, concat_axis=0, tiled=True)
    partial = jnp.sum(partial.astype(jnp.float32), axis=0)
    out = jnp.transpose(partial, (0, 2, 1))
    return out.reshape(out.shape[0], -1) * (1.0 / G)


def solution(mesh):
    placed = (
        P("chan", "tile", None),
        P("chan", None, None, None, None),
        P("chan", "tile", None),
        P("chan", "tile"),
        P("chan", "tile"),
    )
    return jax.shard_map(
        local, mesh=mesh, in_specs=placed, out_specs=P("chan", "tile"), check_vma=False
    )
```

```python
import math

import jax
import jax.numpy as jnp
from jax import lax
from jax.sharding import PartitionSpec as P
from jax.experimental import pallas as pl
from jax.experimental.pallas import tpu as pltpu

G = 8192
S = 64
NW = 32
P_SIZE = 1024
NF = 8


def block_patches(samples, kernel_rows):
    sample_count = samples.shape[1] // 2
    support = kernel_rows.shape[3] // 2
    vis_real = samples[:, :sample_count, None]
    vis_imag = samples[:, sample_count:, None]
    kern_real = kernel_rows[:, 0].astype(jnp.float32)
    kern_imag = kernel_rows[:, 1].astype(jnp.float32)
    full_real = (vis_real * kern_real - vis_imag * kern_imag).astype(jnp.bfloat16)
    full_imag = (vis_real * kern_imag + vis_imag * kern_real).astype(jnp.bfloat16)
    weighted_real = full_real[:, :, support:]
    weighted_imag = full_imag[:, :, support:]
    v_weighted = jnp.stack(
        [
            jnp.concatenate([weighted_real, weighted_imag], axis=-1),
            jnp.concatenate([-weighted_imag, weighted_real], axis=-1),
        ],
        1,
    )
    patch = jnp.einsum("bpkx,bpkn->bxn", kernel_rows, v_weighted, preferred_element_type=jnp.float32)
    return patch[:, :support, :]


PATCH_CHUNK = 128


def patch_kernel(plane_ref, samples_ref, u_ref, v_ref, out_ref):
    base = pl.program_id(0) * PATCH_CHUNK
    for j in range(PATCH_CHUNK):
        w = plane_ref[base + j]
        column = samples_ref[:, j : j + 1]
        vis_real = column[:S]
        vis_imag = column[S:]
        first = v_ref[w, 0].astype(jnp.float32)
        second = v_ref[w, 1].astype(jnp.float32)
        top = (vis_real * first + vis_imag * second).astype(jnp.bfloat16)
        bottom = (vis_real * second - vis_imag * first).astype(jnp.bfloat16)
        rhs = jnp.concatenate(
            [jnp.concatenate([top, bottom], axis=1), jnp.concatenate([bottom, -top], axis=1)], axis=0
        )
        both = jnp.dot(u_ref[w], rhs, preferred_element_type=jnp.float32)
        out_ref[j, 0] = both[:, : 2 * S].astype(jnp.bfloat16)
        out_ref[j, 1] = both[:, 2 * S :].astype(jnp.bfloat16)


def patches_rotated(samples, planes, kernel_set):
    slots = samples.shape[0]
    u_kernel = jnp.transpose(kernel_set[:, :, :, :S], (0, 3, 1, 2)).reshape(NW, S, 2 * S)
    v_real = kernel_set[:, 0, :, S:]
    v_imag = kernel_set[:, 1, :, S:]
    v_parts = jnp.stack(
        [jnp.concatenate([v_real, v_imag], axis=-1), jnp.concatenate([-v_imag, v_real], axis=-1)], axis=1
    )
    grid_spec = pltpu.PrefetchScalarGridSpec(
        num_scalar_prefetch=1,
        grid=(slots // PATCH_CHUNK,),
        in_specs=[
            pl.BlockSpec((2 * S, PATCH_CHUNK), lambda i, p: (0, i)),
            pl.BlockSpec((NW, S, 2 * S), lambda i, p: (0, 0, 0)),
            pl.BlockSpec((NW, 2, S, 2 * S), lambda i, p: (0, 0, 0, 0)),
        ],
        out_specs=pl.BlockSpec((PATCH_CHUNK, 2, S, 2 * S), lambda i, p: (i, 0, 0, 0)),
    )
    return pl.pallas_call(
        patch_kernel,
        grid_spec=grid_spec,
        out_shape=jax.ShapeDtypeStruct((slots, 2, S, 2 * S), jnp.bfloat16),
        cost_estimate=pl.CostEstimate(
            flops=2 * slots * S * 2 * S * 4 * S, transcendentals=0, bytes_accessed=slots * 2 * S * 2 * S * 2 * 2
        ),
    )(planes, jnp.transpose(samples), u_kernel, v_parts)


def phase_index(rows, cols):
    spacing = G // P_SIZE - 1
    return jnp.mod(rows[:, None] * (spacing * cols[None, :]), G)


def cos_sin_f32(index):
    angle = index.astype(jnp.float32) * (2.0 * math.pi / G)
    return jnp.cos(angle), jnp.sin(angle)


def local(visibilities, kernels, destination, cell, plane):
    tile_count = lax.axis_size("tile")
    tile_index = lax.axis_index("tile")
    samples = visibilities[0]
    kernel_set = kernels[0]
    owners = destination[0, :, 0]
    blocks = samples.shape[0]
    capacity = 3 * blocks // tile_count
    spacing = G // P_SIZE - 1

    tiles = jnp.arange(tile_count, dtype=jnp.int32)
    onehot = (owners[:, None] == tiles[None, :]).astype(jnp.int32)
    rank = jnp.sum(jnp.cumsum(onehot, axis=0) * onehot, axis=1) - 1
    slot = jnp.arange(capacity, dtype=jnp.int32)
    pick = (owners[None, None, :] == tiles[:, None, None]) & (rank[None, None, :] == slot[None, :, None])
    pick = pick.astype(jnp.float32).reshape(tile_count * capacity, blocks)
    packed_meta = (cell[0] * NW + plane[0]).astype(jnp.float32)
    routed = jnp.dot(
        pick, jnp.concatenate([samples, packed_meta[:, None]], axis=1), precision=lax.Precision.HIGHEST
    )
    send_samples = routed[:, : samples.shape[1]].reshape(tile_count, capacity, samples.shape[1])
    send_meta = routed[:, samples.shape[1]].reshape(tile_count, capacity)
    meta_row = jnp.pad(send_meta, ((0, 0), (0, samples.shape[1] - capacity)))[:, None, :]
    arrived = lax.all_to_all(
        jnp.concatenate([send_samples, meta_row], axis=1), "tile", split_axis=0, concat_axis=0, tiled=True
    )
    slot_total = tile_count * capacity
    arrived_meta = arrived[:, capacity, :capacity].astype(jnp.int32).reshape(slot_total)
    arrived = arrived[:, :capacity, :].reshape(slot_total, samples.shape[1])

    slab_rows = G // tile_count
    row_cells = slab_rows // S
    cell_cols = G // S
    q_len = G // NF
    q_cells = q_len // S
    j_len = P_SIZE // NF

    cell_r = arrived_meta // NW
    plane_r = arrived_meta % NW
    p2 = patches_rotated(arrived, plane_r, kernel_set).reshape(slot_total * 2, S * 2 * S)

    a_s = cell_r // cell_cols
    cc_s = cell_r % cell_cols
    p_s = cc_s // q_cells
    qc_s = cc_s % q_cells
    resid = jnp.arange(NF, dtype=jnp.int32)
    a_c = jnp.repeat(a_s, 2)[None, :]
    qc_c = jnp.repeat(qc_s, 2)[None, :]
    p_c = jnp.repeat(p_s, 2)[None, :]
    k_c = (jnp.arange(slot_total * 2, dtype=jnp.int32) % 2)[None, :]
    ph_index = jnp.mod(spacing * (p_c - NF // 2) * resid[:, None], NF)
    half = math.sqrt(0.5)
    cos_v = jnp.where(
        ph_index == 0,
        1.0,
        jnp.where(
            ph_index == 4,
            -1.0,
            jnp.where((ph_index == 2) | (ph_index == 6), 0.0, jnp.where((ph_index == 1) | (ph_index == 7), half, -half)),
        ),
    )
    sin_v = jnp.where(
        (ph_index == 0) | (ph_index == 4),
        0.0,
        jnp.where(
            ph_index == 2,
            1.0,
            jnp.where(ph_index == 6, -1.0, jnp.where((ph_index == 1) | (ph_index == 3), half, -half)),
        ),
    )
    phase = jnp.where(k_c == 0, cos_v, sin_v)
    cell_id = jnp.arange(row_cells * q_cells, dtype=jnp.int32)[:, None]
    inside = (a_c == cell_id // q_cells) & (qc_c == cell_id % q_cells)
    l2 = jnp.where(inside[None, :, :], phase[:, None, :], 0.0).astype(jnp.bfloat16)
    l2 = l2.reshape(NF * row_cells * q_cells, slot_total * 2)
    folded = jnp.dot(l2, p2, preferred_element_type=jnp.float32).astype(jnp.bfloat16)
    folded = folded.reshape(NF, row_cells, q_cells, S, 2 * S)

    coarse = jnp.arange(q_cells, dtype=jnp.int32) * S
    fine = jnp.arange(S, dtype=jnp.int32)
    n_full = jnp.arange(2 * j_len, dtype=jnp.int32) % j_len
    j_full = resid[:, None] + NF * (n_full[None, :] - j_len // 2)
    y_full = jnp.arange(2 * S, dtype=jnp.int32) % S
    ca, sa = cos_sin_f32(jnp.mod(coarse[None, :, None] * (spacing * j_full[:, None, :]), G))
    cb, sb = cos_sin_f32(jnp.mod(y_full[None, :, None] * (spacing * j_full[:, None, :]), G))
    ca = ca[:, :, None, :]
    sa = sa[:, :, None, :]
    cb = cb[:, None, :, :]
    sb = sb[:, None, :, :]
    c1 = (ca * cb - sa * sb).astype(jnp.bfloat16)
    s1 = (sa * cb + ca * sb).astype(jnp.bfloat16)
    ri_in = lax.broadcasted_iota(jnp.int32, (1, 1, 2 * S, 2 * j_len), 2) // S
    ri_out = lax.broadcasted_iota(jnp.int32, (1, 1, 2 * S, 2 * j_len), 3) // j_len
    w1 = jnp.where(ri_in == ri_out, c1, jnp.where(ri_in == 0, s1, -s1))
    transformed = jnp.einsum("raqxk,rqkn->raxn", folded, w1, preferred_element_type=jnp.float32)
    transformed = transformed.astype(jnp.bfloat16).reshape(NF, slab_rows, 2, j_len)

    l_index = jnp.arange(P_SIZE, dtype=jnp.int32) - P_SIZE // 2
    row_base = (tile_index * slab_rows - G // 2) + jnp.arange(row_cells, dtype=jnp.int32) * S
    ca, sa = cos_sin_f32(phase_index(l_index, row_base))
    cb, sb = cos_sin_f32(phase_index(l_index, fine))
    c2 = (ca[:, :, None] * cb[:, None, :] - sa[:, :, None] * sb[:, None, :]).astype(jnp.bfloat16)
    s2 = (sa[:, :, None] * cb[:, None, :] + ca[:, :, None] * sb[:, None, :]).astype(jnp.bfloat16)
    c2 = c2.reshape(P_SIZE, slab_rows)
    s2 = s2.reshape(P_SIZE, slab_rows)
    e2 = jnp.stack([c2, -s2], axis=1)
    partial = jnp.einsum("liu,ruij->lrj", e2, transformed, preferred_element_type=jnp.float32)
    chan_count = lax.axis_size("chan")
    partial = partial.reshape(chan_count, P_SIZE // chan_count, NF, j_len)
    partial = lax.all_to_all(partial.astype(jnp.bfloat16), "chan", split_axis=0, concat_axis=0, tiled=True)
    partial = jnp.sum(partial.astype(jnp.float32), axis=0)
    partial = partial.reshape(P_SIZE // chan_count, NF, tile_count, j_len // tile_count)
    partial = jnp.transpose(partial, (2, 0, 1, 3))
    partial = lax.all_to_all(partial.astype(jnp.bfloat16), "tile", split_axis=0, concat_axis=0, tiled=True)
    partial = jnp.sum(partial.astype(jnp.float32), axis=0)
    out = jnp.transpose(partial, (0, 2, 1))
    return out.reshape(out.shape[0], -1) * (1.0 / G)


def solution(mesh):
    placed = (
        P("chan", "tile", None),
        P("chan", None, None, None, None),
        P("chan", "tile", None),
        P("chan", "tile"),
        P("chan", "tile"),
    )
    return jax.shard_map(
        local, mesh=mesh, in_specs=placed, out_specs=P("chan", "tile"), check_vma=False
    )
```

```python
import math

import jax
import jax.numpy as jnp
from jax import lax
from jax.sharding import PartitionSpec as P
from jax.experimental import pallas as pl
from jax.experimental.pallas import tpu as pltpu

G = 8192
S = 64
NW = 32
P_SIZE = 1024
NF = 8


def block_patches(samples, kernel_rows):
    sample_count = samples.shape[1] // 2
    support = kernel_rows.shape[3] // 2
    vis_real = samples[:, :sample_count, None]
    vis_imag = samples[:, sample_count:, None]
    kern_real = kernel_rows[:, 0].astype(jnp.float32)
    kern_imag = kernel_rows[:, 1].astype(jnp.float32)
    full_real = (vis_real * kern_real - vis_imag * kern_imag).astype(jnp.bfloat16)
    full_imag = (vis_real * kern_imag + vis_imag * kern_real).astype(jnp.bfloat16)
    weighted_real = full_real[:, :, support:]
    weighted_imag = full_imag[:, :, support:]
    v_weighted = jnp.stack(
        [
            jnp.concatenate([weighted_real, weighted_imag], axis=-1),
            jnp.concatenate([-weighted_imag, weighted_real], axis=-1),
        ],
        1,
    )
    patch = jnp.einsum("bpkx,bpkn->bxn", kernel_rows, v_weighted, preferred_element_type=jnp.float32)
    return patch[:, :support, :]


PATCH_CHUNK = 128


def patch_kernel(plane_ref, samples_ref, u_ref, v_ref, out_ref):
    base = pl.program_id(0) * PATCH_CHUNK
    for j in range(PATCH_CHUNK):
        w = plane_ref[base + j]
        column = samples_ref[:, j : j + 1]
        vis_real = column[:S]
        vis_imag = column[S:]
        first = v_ref[w, 0].astype(jnp.float32)
        second = v_ref[w, 1].astype(jnp.float32)
        top = (vis_real * first + vis_imag * second).astype(jnp.bfloat16)
        bottom = (vis_real * second - vis_imag * first).astype(jnp.bfloat16)
        rhs = jnp.concatenate(
            [jnp.concatenate([top, bottom], axis=1), jnp.concatenate([bottom, -top], axis=1)], axis=0
        )
        both = jnp.dot(u_ref[w], rhs, preferred_element_type=jnp.float32)
        out_ref[j, 0] = both[:, : 2 * S].astype(jnp.bfloat16)
        out_ref[j, 1] = both[:, 2 * S :].astype(jnp.bfloat16)


def patches_rotated(samples, planes, kernel_set):
    slots = samples.shape[0]
    u_kernel = jnp.transpose(kernel_set[:, :, :, :S], (0, 3, 1, 2)).reshape(NW, S, 2 * S)
    v_real = kernel_set[:, 0, :, S:]
    v_imag = kernel_set[:, 1, :, S:]
    v_parts = jnp.stack(
        [jnp.concatenate([v_real, v_imag], axis=-1), jnp.concatenate([-v_imag, v_real], axis=-1)], axis=1
    )
    grid_spec = pltpu.PrefetchScalarGridSpec(
        num_scalar_prefetch=1,
        grid=(slots // PATCH_CHUNK,),
        in_specs=[
            pl.BlockSpec((2 * S, PATCH_CHUNK), lambda i, p: (0, i)),
            pl.BlockSpec((NW, S, 2 * S), lambda i, p: (0, 0, 0)),
            pl.BlockSpec((NW, 2, S, 2 * S), lambda i, p: (0, 0, 0, 0)),
        ],
        out_specs=pl.BlockSpec((PATCH_CHUNK, 2, S, 2 * S), lambda i, p: (i, 0, 0, 0)),
    )
    return pl.pallas_call(
        patch_kernel,
        grid_spec=grid_spec,
        out_shape=jax.ShapeDtypeStruct((slots, 2, S, 2 * S), jnp.bfloat16),
        cost_estimate=pl.CostEstimate(
            flops=2 * slots * S * 2 * S * 4 * S, transcendentals=0, bytes_accessed=slots * 2 * S * 2 * S * 2 * 2
        ),
    )(planes, jnp.transpose(samples), u_kernel, v_parts)


def phase_index(rows, cols):
    spacing = G // P_SIZE - 1
    return jnp.mod(rows[:, None] * (spacing * cols[None, :]), G)


def cos_sin_f32(index):
    angle = index.astype(jnp.float32) * (2.0 * math.pi / G)
    return jnp.cos(angle), jnp.sin(angle)


def local(visibilities, kernels, destination, cell, plane):
    tile_count = lax.axis_size("tile")
    tile_index = lax.axis_index("tile")
    samples = visibilities[0]
    kernel_set = kernels[0]
    owners = destination[0, :, 0]
    blocks = samples.shape[0]
    capacity = 3 * blocks // tile_count
    spacing = G // P_SIZE - 1

    tiles = jnp.arange(tile_count, dtype=jnp.int32)
    onehot = (owners[:, None] == tiles[None, :]).astype(jnp.int32)
    rank = jnp.sum(jnp.cumsum(onehot, axis=0) * onehot, axis=1) - 1
    slot = jnp.arange(capacity, dtype=jnp.int32)
    pick = (owners[None, None, :] == tiles[:, None, None]) & (rank[None, None, :] == slot[None, :, None])
    pick = pick.astype(jnp.float32).reshape(tile_count * capacity, blocks)
    packed_meta = (cell[0] * NW + plane[0]).astype(jnp.float32)
    routed = jnp.dot(
        pick, jnp.concatenate([samples, packed_meta[:, None]], axis=1), precision=lax.Precision.HIGHEST
    )
    send_samples = routed[:, : samples.shape[1]].reshape(tile_count, capacity, samples.shape[1])
    send_meta = routed[:, samples.shape[1]].reshape(tile_count, capacity)
    meta_row = jnp.pad(send_meta, ((0, 0), (0, samples.shape[1] - capacity)))[:, None, :]
    arrived = lax.all_to_all(
        jnp.concatenate([send_samples, meta_row], axis=1), "tile", split_axis=0, concat_axis=0, tiled=True
    )
    slot_total = tile_count * capacity
    arrived_meta = arrived[:, capacity, :capacity].astype(jnp.int32).reshape(slot_total)
    arrived = arrived[:, :capacity, :].reshape(slot_total, samples.shape[1])

    slab_rows = G // tile_count
    row_cells = slab_rows // S
    cell_cols = G // S
    q_len = G // NF
    q_cells = q_len // S
    j_len = P_SIZE // NF

    cell_r = arrived_meta // NW
    plane_r = arrived_meta % NW
    p2 = patches_rotated(arrived, plane_r, kernel_set).reshape(slot_total * 2, S * 2 * S)

    a_s = cell_r // cell_cols
    cc_s = cell_r % cell_cols
    p_s = cc_s // q_cells
    qc_s = cc_s % q_cells
    resid = jnp.arange(NF, dtype=jnp.int32)
    a_c = jnp.repeat(a_s, 2)[None, :]
    qc_c = jnp.repeat(qc_s, 2)[None, :]
    p_c = jnp.repeat(p_s, 2)[None, :]
    k_c = (jnp.arange(slot_total * 2, dtype=jnp.int32) % 2)[None, :]
    ph_index = jnp.mod(spacing * (p_c - NF // 2) * resid[:, None], NF)
    half = math.sqrt(0.5)
    cos_v = jnp.where(
        ph_index == 0,
        1.0,
        jnp.where(
            ph_index == 4,
            -1.0,
            jnp.where((ph_index == 2) | (ph_index == 6), 0.0, jnp.where((ph_index == 1) | (ph_index == 7), half, -half)),
        ),
    )
    sin_v = jnp.where(
        (ph_index == 0) | (ph_index == 4),
        0.0,
        jnp.where(
            ph_index == 2,
            1.0,
            jnp.where(ph_index == 6, -1.0, jnp.where((ph_index == 1) | (ph_index == 3), half, -half)),
        ),
    )
    phase = jnp.where(k_c == 0, cos_v, sin_v)
    cell_id = jnp.arange(row_cells * q_cells, dtype=jnp.int32)[:, None]
    inside = (a_c == cell_id // q_cells) & (qc_c == cell_id % q_cells)
    l2 = jnp.where(inside[None, :, :], phase[:, None, :], 0.0).astype(jnp.bfloat16)
    l2 = l2.reshape(NF * row_cells * q_cells, slot_total * 2)
    folded = jnp.dot(l2, p2, preferred_element_type=jnp.float32).astype(jnp.bfloat16)
    folded = folded.reshape(NF, row_cells, q_cells, S, 2 * S)

    coarse = jnp.arange(q_cells, dtype=jnp.int32) * S
    fine = jnp.arange(S, dtype=jnp.int32)
    n_full = jnp.arange(2 * j_len, dtype=jnp.int32) % j_len
    j_full = resid[:, None] + NF * (n_full[None, :] - j_len // 2)
    y_full = jnp.arange(2 * S, dtype=jnp.int32) % S
    ca, sa = cos_sin_f32(jnp.mod(coarse[None, :, None] * (spacing * j_full[:, None, :]), G))
    cb, sb = cos_sin_f32(jnp.mod(y_full[None, :, None] * (spacing * j_full[:, None, :]), G))
    ca = ca[:, :, None, :]
    sa = sa[:, :, None, :]
    cb = cb[:, None, :, :]
    sb = sb[:, None, :, :]
    c1 = (ca * cb - sa * sb).astype(jnp.bfloat16)
    s1 = (sa * cb + ca * sb).astype(jnp.bfloat16)
    ri_in = lax.broadcasted_iota(jnp.int32, (1, 1, 2 * S, 2 * j_len), 2) // S
    ri_out = lax.broadcasted_iota(jnp.int32, (1, 1, 2 * S, 2 * j_len), 3) // j_len
    w1 = jnp.where(ri_in == ri_out, c1, jnp.where(ri_in == 0, s1, -s1))
    transformed = jnp.einsum("raqxk,rqkn->raxn", folded, w1, preferred_element_type=jnp.float32)
    transformed = transformed.astype(jnp.bfloat16).reshape(NF, slab_rows, 2 * j_len)

    l_index = jnp.arange(P_SIZE, dtype=jnp.int32) - P_SIZE // 2
    lane_blocks = slab_rows // 128
    block_base = (tile_index * slab_rows - G // 2) + jnp.arange(lane_blocks, dtype=jnp.int32) * 128
    ca, sa = cos_sin_f32(phase_index(l_index, block_base))
    cb, sb = cos_sin_f32(phase_index(l_index, jnp.arange(128, dtype=jnp.int32)))
    c2 = (ca[:, :, None] * cb[:, None, :] - sa[:, :, None] * sb[:, None, :]).astype(jnp.bfloat16)
    s2 = (sa[:, :, None] * cb[:, None, :] + ca[:, :, None] * sb[:, None, :]).astype(jnp.bfloat16)
    c2 = c2.reshape(P_SIZE, slab_rows)
    s2 = s2.reshape(P_SIZE, slab_rows)
    partial = jnp.einsum(
        "lu,ruj->lrj", c2, transformed[:, :, :j_len], preferred_element_type=jnp.float32
    ) - jnp.einsum("lu,ruj->lrj", s2, transformed[:, :, j_len:], preferred_element_type=jnp.float32)
    chan_count = lax.axis_size("chan")
    partial = partial.reshape(chan_count, P_SIZE // chan_count, NF, j_len)
    partial = lax.all_to_all(partial.astype(jnp.bfloat16), "chan", split_axis=0, concat_axis=0, tiled=True)
    partial = jnp.sum(partial.astype(jnp.float32), axis=0)
    partial = partial.reshape(P_SIZE // chan_count, NF, tile_count, j_len // tile_count)
    partial = jnp.transpose(partial, (2, 0, 1, 3))
    partial = lax.all_to_all(partial.astype(jnp.bfloat16), "tile", split_axis=0, concat_axis=0, tiled=True)
    partial = jnp.sum(partial.astype(jnp.float32), axis=0)
    out = jnp.transpose(partial, (0, 2, 1))
    return out.reshape(out.shape[0], -1) * (1.0 / G)


def solution(mesh):
    placed = (
        P("chan", "tile", None),
        P("chan", None, None, None, None),
        P("chan", "tile", None),
        P("chan", "tile"),
        P("chan", "tile"),
    )
    return jax.shard_map(
        local, mesh=mesh, in_specs=placed, out_specs=P("chan", "tile"), check_vma=False
    )
```

```python
import math

import jax
import jax.numpy as jnp
from jax import lax
from jax.sharding import PartitionSpec as P
from jax.experimental import pallas as pl
from jax.experimental.pallas import tpu as pltpu

G = 8192
S = 64
NW = 32
P_SIZE = 1024
NF = 8


def block_patches(samples, kernel_rows):
    sample_count = samples.shape[1] // 2
    support = kernel_rows.shape[3] // 2
    vis_real = samples[:, :sample_count, None]
    vis_imag = samples[:, sample_count:, None]
    kern_real = kernel_rows[:, 0].astype(jnp.float32)
    kern_imag = kernel_rows[:, 1].astype(jnp.float32)
    full_real = (vis_real * kern_real - vis_imag * kern_imag).astype(jnp.bfloat16)
    full_imag = (vis_real * kern_imag + vis_imag * kern_real).astype(jnp.bfloat16)
    weighted_real = full_real[:, :, support:]
    weighted_imag = full_imag[:, :, support:]
    v_weighted = jnp.stack(
        [
            jnp.concatenate([weighted_real, weighted_imag], axis=-1),
            jnp.concatenate([-weighted_imag, weighted_real], axis=-1),
        ],
        1,
    )
    patch = jnp.einsum("bpkx,bpkn->bxn", kernel_rows, v_weighted, preferred_element_type=jnp.float32)
    return patch[:, :support, :]


PATCH_CHUNK = 128


def patch_kernel(plane_ref, samples_ref, u_ref, v_ref, out_ref):
    base = pl.program_id(0) * PATCH_CHUNK
    for j in range(PATCH_CHUNK):
        w = plane_ref[base + j]
        column = samples_ref[:, j : j + 1]
        vis_real = column[:S]
        vis_imag = column[S:]
        first = v_ref[w, 0].astype(jnp.float32)
        second = v_ref[w, 1].astype(jnp.float32)
        top = (vis_real * first + vis_imag * second).astype(jnp.bfloat16)
        bottom = (vis_real * second - vis_imag * first).astype(jnp.bfloat16)
        rhs = jnp.concatenate(
            [jnp.concatenate([top, bottom], axis=1), jnp.concatenate([bottom, -top], axis=1)], axis=0
        )
        both = jnp.dot(u_ref[w], rhs, preferred_element_type=jnp.float32)
        out_ref[j, 0] = both[:, : 2 * S].astype(jnp.bfloat16)
        out_ref[j, 1] = both[:, 2 * S :].astype(jnp.bfloat16)


def patches_rotated(samples, planes, kernel_set):
    slots = samples.shape[0]
    u_kernel = jnp.transpose(kernel_set[:, :, :, :S], (0, 3, 1, 2)).reshape(NW, S, 2 * S)
    v_real = kernel_set[:, 0, :, S:]
    v_imag = kernel_set[:, 1, :, S:]
    v_parts = jnp.stack(
        [jnp.concatenate([v_real, v_imag], axis=-1), jnp.concatenate([-v_imag, v_real], axis=-1)], axis=1
    )
    grid_spec = pltpu.PrefetchScalarGridSpec(
        num_scalar_prefetch=1,
        grid=(slots // PATCH_CHUNK,),
        in_specs=[
            pl.BlockSpec((2 * S, PATCH_CHUNK), lambda i, p: (0, i)),
            pl.BlockSpec((NW, S, 2 * S), lambda i, p: (0, 0, 0)),
            pl.BlockSpec((NW, 2, S, 2 * S), lambda i, p: (0, 0, 0, 0)),
        ],
        out_specs=pl.BlockSpec((PATCH_CHUNK, 2, S, 2 * S), lambda i, p: (i, 0, 0, 0)),
    )
    return pl.pallas_call(
        patch_kernel,
        grid_spec=grid_spec,
        out_shape=jax.ShapeDtypeStruct((slots, 2, S, 2 * S), jnp.bfloat16),
        cost_estimate=pl.CostEstimate(
            flops=2 * slots * S * 2 * S * 4 * S, transcendentals=0, bytes_accessed=slots * 2 * S * 2 * S * 2 * 2
        ),
    )(planes, jnp.transpose(samples), u_kernel, v_parts)


def phase_index(rows, cols):
    spacing = G // P_SIZE - 1
    return jnp.mod(rows[:, None] * (spacing * cols[None, :]), G)


def cos_sin_f32(index):
    angle = index.astype(jnp.float32) * (2.0 * math.pi / G)
    return jnp.cos(angle), jnp.sin(angle)


def local(visibilities, kernels, destination, cell, plane):
    tile_count = lax.axis_size("tile")
    tile_index = lax.axis_index("tile")
    samples = visibilities[0]
    kernel_set = kernels[0]
    owners = destination[0, :, 0]
    blocks = samples.shape[0]
    capacity = 3 * blocks // tile_count
    spacing = G // P_SIZE - 1

    tiles = jnp.arange(tile_count, dtype=jnp.int32)
    onehot = (owners[:, None] == tiles[None, :]).astype(jnp.int32)
    rank = jnp.sum(jnp.cumsum(onehot, axis=0) * onehot, axis=1) - 1
    slot = jnp.arange(capacity, dtype=jnp.int32)
    pick = (owners[None, None, :] == tiles[:, None, None]) & (rank[None, None, :] == slot[None, :, None])
    pick = pick.astype(jnp.float32).reshape(tile_count * capacity, blocks)
    packed_meta = (cell[0] * NW + plane[0]).astype(jnp.float32)
    routed = jnp.dot(
        pick, jnp.concatenate([samples, packed_meta[:, None]], axis=1), precision=lax.Precision.HIGHEST
    )
    send_samples = routed[:, : samples.shape[1]].reshape(tile_count, capacity, samples.shape[1])
    send_meta = routed[:, samples.shape[1]].reshape(tile_count, capacity)
    meta_row = jnp.pad(send_meta, ((0, 0), (0, samples.shape[1] - capacity)))[:, None, :]
    arrived = lax.all_to_all(
        jnp.concatenate([send_samples, meta_row], axis=1), "tile", split_axis=0, concat_axis=0, tiled=True
    )
    slot_total = tile_count * capacity
    arrived_meta = arrived[:, capacity, :capacity].astype(jnp.int32).reshape(slot_total)
    arrived = arrived[:, :capacity, :].reshape(slot_total, samples.shape[1])

    slab_rows = G // tile_count
    row_cells = slab_rows // S
    cell_cols = G // S
    q_len = G // NF
    q_cells = q_len // S
    j_len = P_SIZE // NF

    cell_r = arrived_meta // NW
    plane_r = arrived_meta % NW
    p2 = patches_rotated(arrived, plane_r, kernel_set).reshape(slot_total * 2, S * 2 * S)

    a_s = cell_r // cell_cols
    cc_s = cell_r % cell_cols
    p_s = cc_s // q_cells
    qc_s = cc_s % q_cells
    resid = jnp.arange(NF, dtype=jnp.int32)
    a_c = jnp.repeat(a_s, 2)[None, :]
    qc_c = jnp.repeat(qc_s, 2)[None, :]
    p_c = jnp.repeat(p_s, 2)[None, :]
    k_c = (jnp.arange(slot_total * 2, dtype=jnp.int32) % 2)[None, :]
    ph_index = jnp.mod(spacing * (p_c - NF // 2) * resid[:, None], NF)
    half = math.sqrt(0.5)
    cos_v = jnp.where(
        ph_index == 0,
        1.0,
        jnp.where(
            ph_index == 4,
            -1.0,
            jnp.where((ph_index == 2) | (ph_index == 6), 0.0, jnp.where((ph_index == 1) | (ph_index == 7), half, -half)),
        ),
    )
    sin_v = jnp.where(
        (ph_index == 0) | (ph_index == 4),
        0.0,
        jnp.where(
            ph_index == 2,
            1.0,
            jnp.where(ph_index == 6, -1.0, jnp.where((ph_index == 1) | (ph_index == 3), half, -half)),
        ),
    )
    phase = jnp.where(k_c == 0, cos_v, sin_v)
    cell_id = jnp.arange(row_cells * q_cells, dtype=jnp.int32)[:, None]
    inside = (a_c == cell_id // q_cells) & (qc_c == cell_id % q_cells)
    l2 = jnp.where(inside[None, :, :], phase[:, None, :], 0.0).astype(jnp.bfloat16)
    l2 = l2.reshape(NF * row_cells * q_cells, slot_total * 2)
    folded = jnp.dot(l2, p2, preferred_element_type=jnp.float32).astype(jnp.bfloat16)
    folded = folded.reshape(NF, row_cells, q_cells, S, 2 * S)

    coarse = jnp.arange(q_cells, dtype=jnp.int32) * S
    fine = jnp.arange(S, dtype=jnp.int32)
    n_full = jnp.arange(2 * j_len, dtype=jnp.int32) % j_len
    j_full = resid[:, None] + NF * (n_full[None, :] - j_len // 2)
    y_full = jnp.arange(2 * S, dtype=jnp.int32) % S
    ca, sa = cos_sin_f32(jnp.mod(coarse[None, :, None] * (spacing * j_full[:, None, :]), G))
    cb, sb = cos_sin_f32(jnp.mod(y_full[None, :, None] * (spacing * j_full[:, None, :]), G))
    ca = ca[:, :, None, :]
    sa = sa[:, :, None, :]
    cb = cb[:, None, :, :]
    sb = sb[:, None, :, :]
    c1 = (ca * cb - sa * sb).astype(jnp.bfloat16)
    s1 = (sa * cb + ca * sb).astype(jnp.bfloat16)
    ri_in = lax.broadcasted_iota(jnp.int32, (1, 1, 2 * S, 2 * j_len), 2) // S
    ri_out = lax.broadcasted_iota(jnp.int32, (1, 1, 2 * S, 2 * j_len), 3) // j_len
    w1 = jnp.where(ri_in == ri_out, c1, jnp.where(ri_in == 0, s1, -s1))
    transformed = jnp.einsum("raqxk,rqkn->raxn", folded, w1, preferred_element_type=jnp.float32)
    transformed = transformed.astype(jnp.bfloat16).reshape(NF, slab_rows, 2 * j_len)

    l_index = jnp.arange(P_SIZE, dtype=jnp.int32) - P_SIZE // 2
    lane_blocks = slab_rows // 128
    block_base = (tile_index * slab_rows - G // 2) + jnp.arange(lane_blocks, dtype=jnp.int32) * 128
    ca, sa = cos_sin_f32(phase_index(l_index, block_base))
    cb, sb = cos_sin_f32(phase_index(l_index, jnp.arange(128, dtype=jnp.int32)))
    c2 = (ca[:, :, None] * cb[:, None, :] - sa[:, :, None] * sb[:, None, :]).astype(jnp.bfloat16)
    s2 = (sa[:, :, None] * cb[:, None, :] + ca[:, :, None] * sb[:, None, :]).astype(jnp.bfloat16)
    c2 = c2.reshape(P_SIZE, slab_rows)
    s2 = s2.reshape(P_SIZE, slab_rows)
    partial = jnp.einsum(
        "lu,ruj->lrj", c2, transformed[:, :, :j_len], preferred_element_type=jnp.float32
    ) - jnp.einsum("lu,ruj->lrj", s2, transformed[:, :, j_len:], preferred_element_type=jnp.float32)
    chan_count = lax.axis_size("chan")
    partial = partial.reshape(chan_count, P_SIZE // chan_count, NF, tile_count, j_len // tile_count)
    partial = jnp.transpose(partial, (0, 3, 1, 2, 4)).reshape(
        chan_count * tile_count, P_SIZE // chan_count, NF, j_len // tile_count
    )
    partial = lax.all_to_all(
        partial.astype(jnp.bfloat16), ("chan", "tile"), split_axis=0, concat_axis=0, tiled=True
    )
    partial = jnp.sum(partial.astype(jnp.float32), axis=0)
    out = jnp.transpose(partial, (0, 2, 1))
    return out.reshape(out.shape[0], -1) * (1.0 / G)


def solution(mesh):
    placed = (
        P("chan", "tile", None),
        P("chan", None, None, None, None),
        P("chan", "tile", None),
        P("chan", "tile"),
        P("chan", "tile"),
    )
    return jax.shard_map(
        local, mesh=mesh, in_specs=placed, out_specs=P("chan", "tile"), check_vma=False
    )
```

```python
import math

import jax
import jax.numpy as jnp
from jax import lax
from jax.sharding import PartitionSpec as P
from jax.experimental import pallas as pl
from jax.experimental.pallas import tpu as pltpu

G = 8192
S = 64
NW = 32
P_SIZE = 1024
NF = 8


def block_patches(samples, kernel_rows):
    sample_count = samples.shape[1] // 2
    support = kernel_rows.shape[3] // 2
    vis_real = samples[:, :sample_count, None]
    vis_imag = samples[:, sample_count:, None]
    kern_real = kernel_rows[:, 0].astype(jnp.float32)
    kern_imag = kernel_rows[:, 1].astype(jnp.float32)
    full_real = (vis_real * kern_real - vis_imag * kern_imag).astype(jnp.bfloat16)
    full_imag = (vis_real * kern_imag + vis_imag * kern_real).astype(jnp.bfloat16)
    weighted_real = full_real[:, :, support:]
    weighted_imag = full_imag[:, :, support:]
    v_weighted = jnp.stack(
        [
            jnp.concatenate([weighted_real, weighted_imag], axis=-1),
            jnp.concatenate([-weighted_imag, weighted_real], axis=-1),
        ],
        1,
    )
    patch = jnp.einsum("bpkx,bpkn->bxn", kernel_rows, v_weighted, preferred_element_type=jnp.float32)
    return patch[:, :support, :]


PATCH_CHUNK = 128


def patch_kernel(plane_ref, samples_ref, u_ref, v_ref, out_ref):
    base = pl.program_id(0) * PATCH_CHUNK
    for j in range(PATCH_CHUNK):
        w = plane_ref[base + j]
        column = samples_ref[:, j : j + 1]
        vis_real = column[:S]
        vis_imag = column[S:]
        first = v_ref[w, 0].astype(jnp.float32)
        second = v_ref[w, 1].astype(jnp.float32)
        top = (vis_real * first + vis_imag * second).astype(jnp.bfloat16)
        bottom = (vis_real * second - vis_imag * first).astype(jnp.bfloat16)
        rhs = jnp.concatenate(
            [jnp.concatenate([top, bottom], axis=1), jnp.concatenate([bottom, -top], axis=1)], axis=0
        )
        both = jnp.dot(u_ref[w], rhs, preferred_element_type=jnp.float32)
        out_ref[j, 0] = both[:, : 2 * S].astype(jnp.bfloat16)
        out_ref[j, 1] = both[:, 2 * S :].astype(jnp.bfloat16)


def patches_rotated(samples, planes, kernel_set):
    slots = samples.shape[0]
    u_kernel = jnp.transpose(kernel_set[:, :, :, :S], (0, 3, 1, 2)).reshape(NW, S, 2 * S)
    v_real = kernel_set[:, 0, :, S:]
    v_imag = kernel_set[:, 1, :, S:]
    v_parts = jnp.stack(
        [jnp.concatenate([v_real, v_imag], axis=-1), jnp.concatenate([-v_imag, v_real], axis=-1)], axis=1
    )
    grid_spec = pltpu.PrefetchScalarGridSpec(
        num_scalar_prefetch=1,
        grid=(slots // PATCH_CHUNK,),
        in_specs=[
            pl.BlockSpec((2 * S, PATCH_CHUNK), lambda i, p: (0, i)),
            pl.BlockSpec((NW, S, 2 * S), lambda i, p: (0, 0, 0)),
            pl.BlockSpec((NW, 2, S, 2 * S), lambda i, p: (0, 0, 0, 0)),
        ],
        out_specs=pl.BlockSpec((PATCH_CHUNK, 2, S, 2 * S), lambda i, p: (i, 0, 0, 0)),
    )
    return pl.pallas_call(
        patch_kernel,
        grid_spec=grid_spec,
        out_shape=jax.ShapeDtypeStruct((slots, 2, S, 2 * S), jnp.bfloat16),
        cost_estimate=pl.CostEstimate(
            flops=2 * slots * S * 2 * S * 4 * S, transcendentals=0, bytes_accessed=slots * 2 * S * 2 * S * 2 * 2
        ),
    )(planes, jnp.transpose(samples), u_kernel, v_parts)


def phase_index(rows, cols):
    spacing = G // P_SIZE - 1
    return jnp.mod(rows[:, None] * (spacing * cols[None, :]), G)


def cos_sin_f32(index):
    angle = index.astype(jnp.float32) * (2.0 * math.pi / G)
    return jnp.cos(angle), jnp.sin(angle)


def local(visibilities, kernels, destination, cell, plane):
    tile_count = lax.axis_size("tile")
    tile_index = lax.axis_index("tile")
    samples = visibilities[0]
    kernel_set = kernels[0]
    owners = destination[0, :, 0]
    blocks = samples.shape[0]
    capacity = 3 * blocks // tile_count
    spacing = G // P_SIZE - 1

    tiles = jnp.arange(tile_count, dtype=jnp.int32)
    onehot = (owners[:, None] == tiles[None, :]).astype(jnp.int32)
    rank = jnp.sum(jnp.cumsum(onehot, axis=0) * onehot, axis=1) - 1
    slot = jnp.arange(capacity, dtype=jnp.int32)
    pick = (owners[None, None, :] == tiles[:, None, None]) & (rank[None, None, :] == slot[None, :, None])
    pick = pick.astype(jnp.float32).reshape(tile_count * capacity, blocks)
    packed_meta = (cell[0] * NW + plane[0]).astype(jnp.float32)
    routed = jnp.dot(
        pick, jnp.concatenate([samples, packed_meta[:, None]], axis=1), precision=lax.Precision.HIGHEST
    )
    send_samples = routed[:, : samples.shape[1]].reshape(tile_count, capacity, samples.shape[1])
    send_meta = routed[:, samples.shape[1]].reshape(tile_count, capacity)
    meta_row = jnp.pad(send_meta, ((0, 0), (0, samples.shape[1] - capacity)))[:, None, :]
    arrived = lax.all_to_all(
        jnp.concatenate([send_samples, meta_row], axis=1), "tile", split_axis=0, concat_axis=0, tiled=True
    )
    slot_total = tile_count * capacity
    arrived_meta = arrived[:, capacity, :capacity].astype(jnp.int32).reshape(slot_total)
    arrived = arrived[:, :capacity, :].reshape(slot_total, samples.shape[1])

    slab_rows = G // tile_count
    row_cells = slab_rows // S
    cell_cols = G // S
    q_len = G // NF
    q_cells = q_len // S
    j_len = P_SIZE // NF

    cell_r = arrived_meta // NW
    plane_r = arrived_meta % NW
    p2 = patches_rotated(arrived, plane_r, kernel_set).reshape(slot_total * 2, S * 2 * S)

    a_s = cell_r // cell_cols
    cc_s = cell_r % cell_cols
    p_s = cc_s // q_cells
    qc_s = cc_s % q_cells
    resid = jnp.arange(NF, dtype=jnp.int32)
    a_c = jnp.repeat(a_s, 2)[None, :]
    qc_c = jnp.repeat(qc_s, 2)[None, :]
    p_c = jnp.repeat(p_s, 2)[None, :]
    k_c = (jnp.arange(slot_total * 2, dtype=jnp.int32) % 2)[None, :]
    ph_index = jnp.mod(spacing * (p_c - NF // 2) * resid[:, None], NF)
    half = math.sqrt(0.5)
    cos_v = jnp.where(
        ph_index == 0,
        1.0,
        jnp.where(
            ph_index == 4,
            -1.0,
            jnp.where((ph_index == 2) | (ph_index == 6), 0.0, jnp.where((ph_index == 1) | (ph_index == 7), half, -half)),
        ),
    )
    sin_v = jnp.where(
        (ph_index == 0) | (ph_index == 4),
        0.0,
        jnp.where(
            ph_index == 2,
            1.0,
            jnp.where(ph_index == 6, -1.0, jnp.where((ph_index == 1) | (ph_index == 3), half, -half)),
        ),
    )
    phase = jnp.where(k_c == 0, cos_v, sin_v)
    cell_id = jnp.arange(row_cells * q_cells, dtype=jnp.int32)[:, None]
    inside = (a_c == cell_id // q_cells) & (qc_c == cell_id % q_cells)
    l2 = jnp.where(inside[None, :, :], phase[:, None, :], 0.0).astype(jnp.bfloat16)
    l2 = l2.reshape(NF * row_cells * q_cells, slot_total * 2)
    folded = jnp.dot(l2, p2, preferred_element_type=jnp.float32).astype(jnp.bfloat16)
    folded = folded.reshape(NF, row_cells, q_cells // 8, 8, S, 2 * S)

    coarse = jnp.arange(q_cells, dtype=jnp.int32) * S
    fine = jnp.arange(S, dtype=jnp.int32)
    n_full = jnp.arange(2 * j_len, dtype=jnp.int32) % j_len
    j_full = resid[:, None] + NF * (n_full[None, :] - j_len // 2)
    y_full = jnp.arange(2 * S, dtype=jnp.int32) % S
    ca, sa = cos_sin_f32(jnp.mod(coarse[None, :, None] * (spacing * j_full[:, None, :]), G))
    cb, sb = cos_sin_f32(jnp.mod(y_full[None, :, None] * (spacing * j_full[:, None, :]), G))
    ca = ca[:, :, None, :]
    sa = sa[:, :, None, :]
    cb = cb[:, None, :, :]
    sb = sb[:, None, :, :]
    c1 = (ca * cb - sa * sb).astype(jnp.bfloat16)
    s1 = (sa * cb + ca * sb).astype(jnp.bfloat16)
    ri_in = lax.broadcasted_iota(jnp.int32, (1, 1, 2 * S, 2 * j_len), 2) // S
    ri_out = lax.broadcasted_iota(jnp.int32, (1, 1, 2 * S, 2 * j_len), 3) // j_len
    w1 = jnp.where(ri_in == ri_out, c1, jnp.where(ri_in == 0, s1, -s1))
    transformed = jnp.einsum("rahqxk,rhqkn->raxn", folded, w1.reshape(NF, q_cells // 8, 8, 2 * S, 2 * j_len), preferred_element_type=jnp.float32)
    transformed = transformed.astype(jnp.bfloat16).reshape(NF, slab_rows, 2 * j_len)

    l_index = jnp.arange(P_SIZE, dtype=jnp.int32) - P_SIZE // 2
    lane_blocks = slab_rows // 128
    block_base = (tile_index * slab_rows - G // 2) + jnp.arange(lane_blocks, dtype=jnp.int32) * 128
    ca, sa = cos_sin_f32(phase_index(l_index, block_base))
    cb, sb = cos_sin_f32(phase_index(l_index, jnp.arange(128, dtype=jnp.int32)))
    c2 = (ca[:, :, None] * cb[:, None, :] - sa[:, :, None] * sb[:, None, :]).astype(jnp.bfloat16)
    s2 = (sa[:, :, None] * cb[:, None, :] + ca[:, :, None] * sb[:, None, :]).astype(jnp.bfloat16)
    c2 = c2.reshape(P_SIZE, slab_rows)
    s2 = s2.reshape(P_SIZE, slab_rows)
    partial = jnp.einsum(
        "lu,ruj->lrj", c2, transformed[:, :, :j_len], preferred_element_type=jnp.float32
    ) - jnp.einsum("lu,ruj->lrj", s2, transformed[:, :, j_len:], preferred_element_type=jnp.float32)
    chan_count = lax.axis_size("chan")
    partial = partial.reshape(chan_count, P_SIZE // chan_count, NF, j_len)
    partial = lax.all_to_all(partial.astype(jnp.bfloat16), "chan", split_axis=0, concat_axis=0, tiled=True)
    partial = jnp.sum(partial.astype(jnp.float32), axis=0)
    partial = partial.reshape(P_SIZE // chan_count, NF, tile_count, j_len // tile_count)
    partial = jnp.transpose(partial, (2, 0, 1, 3))
    partial = lax.all_to_all(partial.astype(jnp.bfloat16), "tile", split_axis=0, concat_axis=0, tiled=True)
    partial = jnp.sum(partial.astype(jnp.float32), axis=0)
    out = jnp.transpose(partial, (0, 2, 1))
    return out.reshape(out.shape[0], -1) * (1.0 / G)


def solution(mesh):
    placed = (
        P("chan", "tile", None),
        P("chan", None, None, None, None),
        P("chan", "tile", None),
        P("chan", "tile"),
        P("chan", "tile"),
    )
    return jax.shard_map(
        local, mesh=mesh, in_specs=placed, out_specs=P("chan", "tile"), check_vma=False
    )
```

```python
import math

import jax
import jax.numpy as jnp
from jax import lax
from jax.sharding import PartitionSpec as P
from jax.experimental import pallas as pl
from jax.experimental.pallas import tpu as pltpu

G = 8192
S = 64
NW = 32
P_SIZE = 1024
NF = 8


def block_patches(samples, kernel_rows):
    sample_count = samples.shape[1] // 2
    support = kernel_rows.shape[3] // 2
    vis_real = samples[:, :sample_count, None]
    vis_imag = samples[:, sample_count:, None]
    kern_real = kernel_rows[:, 0].astype(jnp.float32)
    kern_imag = kernel_rows[:, 1].astype(jnp.float32)
    full_real = (vis_real * kern_real - vis_imag * kern_imag).astype(jnp.bfloat16)
    full_imag = (vis_real * kern_imag + vis_imag * kern_real).astype(jnp.bfloat16)
    weighted_real = full_real[:, :, support:]
    weighted_imag = full_imag[:, :, support:]
    v_weighted = jnp.stack(
        [
            jnp.concatenate([weighted_real, weighted_imag], axis=-1),
            jnp.concatenate([-weighted_imag, weighted_real], axis=-1),
        ],
        1,
    )
    patch = jnp.einsum("bpkx,bpkn->bxn", kernel_rows, v_weighted, preferred_element_type=jnp.float32)
    return patch[:, :support, :]


PATCH_CHUNK = 128


def patch_kernel(plane_ref, samples_ref, u_ref, v_ref, out_ref):
    base = pl.program_id(0) * PATCH_CHUNK
    for j in range(PATCH_CHUNK):
        w = plane_ref[base + j]
        column = samples_ref[:, j : j + 1]
        vis_real = column[:S]
        vis_imag = column[S:]
        first = v_ref[w, 0].astype(jnp.float32)
        second = v_ref[w, 1].astype(jnp.float32)
        top = (vis_real * first + vis_imag * second).astype(jnp.bfloat16)
        bottom = (vis_real * second - vis_imag * first).astype(jnp.bfloat16)
        rhs = jnp.concatenate(
            [jnp.concatenate([top, bottom], axis=1), jnp.concatenate([bottom, -top], axis=1)], axis=0
        )
        both = jnp.dot(u_ref[w], rhs, preferred_element_type=jnp.float32)
        out_ref[j, 0] = both[:, : 2 * S].astype(jnp.bfloat16)
        out_ref[j, 1] = both[:, 2 * S :].astype(jnp.bfloat16)


def patches_rotated(samples, planes, kernel_set):
    slots = samples.shape[0]
    u_kernel = jnp.transpose(kernel_set[:, :, :, :S], (0, 3, 1, 2)).reshape(NW, S, 2 * S)
    v_real = kernel_set[:, 0, :, S:]
    v_imag = kernel_set[:, 1, :, S:]
    v_parts = jnp.stack(
        [jnp.concatenate([v_real, v_imag], axis=-1), jnp.concatenate([-v_imag, v_real], axis=-1)], axis=1
    )
    grid_spec = pltpu.PrefetchScalarGridSpec(
        num_scalar_prefetch=1,
        grid=(slots // PATCH_CHUNK,),
        in_specs=[
            pl.BlockSpec((2 * S, PATCH_CHUNK), lambda i, p: (0, i)),
            pl.BlockSpec((NW, S, 2 * S), lambda i, p: (0, 0, 0)),
            pl.BlockSpec((NW, 2, S, 2 * S), lambda i, p: (0, 0, 0, 0)),
        ],
        out_specs=pl.BlockSpec((PATCH_CHUNK, 2, S, 2 * S), lambda i, p: (i, 0, 0, 0)),
    )
    return pl.pallas_call(
        patch_kernel,
        grid_spec=grid_spec,
        out_shape=jax.ShapeDtypeStruct((slots, 2, S, 2 * S), jnp.bfloat16),
        cost_estimate=pl.CostEstimate(
            flops=2 * slots * S * 2 * S * 4 * S, transcendentals=0, bytes_accessed=slots * 2 * S * 2 * S * 2 * 2
        ),
    )(planes, jnp.transpose(samples), u_kernel, v_parts)


def phase_index(rows, cols):
    spacing = G // P_SIZE - 1
    return jnp.mod(rows[:, None] * (spacing * cols[None, :]), G)


def cos_sin_f32(index):
    angle = index.astype(jnp.float32) * (2.0 * math.pi / G)
    return jnp.cos(angle), jnp.sin(angle)


def local(visibilities, kernels, destination, cell, plane):
    tile_count = lax.axis_size("tile")
    tile_index = lax.axis_index("tile")
    samples = visibilities[0]
    kernel_set = kernels[0]
    owners = destination[0, :, 0]
    blocks = samples.shape[0]
    capacity = 3 * blocks // tile_count
    spacing = G // P_SIZE - 1

    tiles = jnp.arange(tile_count, dtype=jnp.int32)
    onehot = (owners[:, None] == tiles[None, :]).astype(jnp.int32)
    rank = jnp.sum(jnp.cumsum(onehot, axis=0) * onehot, axis=1) - 1
    slot = jnp.arange(capacity, dtype=jnp.int32)
    pick = (owners[None, None, :] == tiles[:, None, None]) & (rank[None, None, :] == slot[None, :, None])
    pick = pick.astype(jnp.float32).reshape(tile_count * capacity, blocks)
    packed_meta = (cell[0] * NW + plane[0]).astype(jnp.float32)
    routed = jnp.dot(
        pick, jnp.concatenate([samples, packed_meta[:, None]], axis=1), precision=lax.Precision.HIGHEST
    )
    send_samples = routed[:, : samples.shape[1]].reshape(tile_count, capacity, samples.shape[1])
    send_meta = routed[:, samples.shape[1]].reshape(tile_count, capacity)
    meta_row = jnp.pad(send_meta, ((0, 0), (0, samples.shape[1] - capacity)))[:, None, :]
    arrived = lax.all_to_all(
        jnp.concatenate([send_samples, meta_row], axis=1), "tile", split_axis=0, concat_axis=0, tiled=True
    )
    slot_total = tile_count * capacity
    arrived_meta = arrived[:, capacity, :capacity].astype(jnp.int32).reshape(slot_total)
    arrived = arrived[:, :capacity, :].reshape(slot_total, samples.shape[1])

    slab_rows = G // tile_count
    row_cells = slab_rows // S
    cell_cols = G // S
    q_len = G // NF
    q_cells = q_len // S
    j_len = P_SIZE // NF

    cell_r = arrived_meta // NW
    plane_r = arrived_meta % NW
    p2 = patches_rotated(arrived, plane_r, kernel_set).reshape(slot_total * 2, S * 2 * S)

    a_s = cell_r // cell_cols
    cc_s = cell_r % cell_cols
    p_s = cc_s // q_cells
    qc_s = cc_s % q_cells
    resid = jnp.arange(NF, dtype=jnp.int32)
    a_c = jnp.repeat(a_s, 2)[None, :]
    qc_c = jnp.repeat(qc_s, 2)[None, :]
    p_c = jnp.repeat(p_s, 2)[None, :]
    k_c = (jnp.arange(slot_total * 2, dtype=jnp.int32) % 2)[None, :]
    ph_index = jnp.mod(spacing * (p_c - NF // 2) * resid[:, None], NF)
    half = math.sqrt(0.5)
    cos_v = jnp.where(
        ph_index == 0,
        1.0,
        jnp.where(
            ph_index == 4,
            -1.0,
            jnp.where((ph_index == 2) | (ph_index == 6), 0.0, jnp.where((ph_index == 1) | (ph_index == 7), half, -half)),
        ),
    )
    sin_v = jnp.where(
        (ph_index == 0) | (ph_index == 4),
        0.0,
        jnp.where(
            ph_index == 2,
            1.0,
            jnp.where(ph_index == 6, -1.0, jnp.where((ph_index == 1) | (ph_index == 3), half, -half)),
        ),
    )
    phase = jnp.where(k_c == 0, cos_v, sin_v)
    cell_id = jnp.arange(row_cells * q_cells, dtype=jnp.int32)[:, None]
    inside = (a_c == cell_id // q_cells) & (qc_c == cell_id % q_cells)
    l2 = jnp.where(inside[None, :, :], phase[:, None, :], 0.0).astype(jnp.bfloat16)
    l2 = l2.reshape(NF * row_cells * q_cells, slot_total * 2)
    folded = jnp.dot(l2, p2, preferred_element_type=jnp.float32).astype(jnp.bfloat16)
    folded = folded.reshape(NF, row_cells, q_cells // 8, 8, S, 2 * S)

    coarse = jnp.arange(q_cells, dtype=jnp.int32) * S
    fine = jnp.arange(S, dtype=jnp.int32)
    n_full = jnp.arange(2 * j_len, dtype=jnp.int32) % j_len
    j_full = resid[:, None] + NF * (n_full[None, :] - j_len // 2)
    y_full = jnp.arange(2 * S, dtype=jnp.int32) % S
    ca, sa = cos_sin_f32(jnp.mod(coarse[None, :, None] * (spacing * j_full[:, None, :]), G))
    cb, sb = cos_sin_f32(jnp.mod(y_full[None, :, None] * (spacing * j_full[:, None, :]), G))
    ca, sa, cb, sb = lax.optimization_barrier((ca, sa, cb, sb))
    ca = ca[:, :, None, :]
    sa = sa[:, :, None, :]
    cb = cb[:, None, :, :]
    sb = sb[:, None, :, :]
    c1 = (ca * cb - sa * sb).astype(jnp.bfloat16)
    s1 = (sa * cb + ca * sb).astype(jnp.bfloat16)
    ri_in = lax.broadcasted_iota(jnp.int32, (1, 1, 2 * S, 2 * j_len), 2) // S
    ri_out = lax.broadcasted_iota(jnp.int32, (1, 1, 2 * S, 2 * j_len), 3) // j_len
    w1 = jnp.where(ri_in == ri_out, c1, jnp.where(ri_in == 0, s1, -s1))
    transformed = jnp.einsum("rahqxk,rhqkn->raxn", folded, w1.reshape(NF, q_cells // 8, 8, 2 * S, 2 * j_len), preferred_element_type=jnp.float32)
    transformed = transformed.astype(jnp.bfloat16).reshape(NF, slab_rows, 2 * j_len)

    l_index = jnp.arange(P_SIZE, dtype=jnp.int32) - P_SIZE // 2
    lane_blocks = slab_rows // 128
    block_base = (tile_index * slab_rows - G // 2) + jnp.arange(lane_blocks, dtype=jnp.int32) * 128
    ca, sa = cos_sin_f32(phase_index(l_index, block_base))
    cb, sb = cos_sin_f32(phase_index(l_index, jnp.arange(128, dtype=jnp.int32)))
    ca, sa, cb, sb = lax.optimization_barrier((ca, sa, cb, sb))
    c2 = (ca[:, :, None] * cb[:, None, :] - sa[:, :, None] * sb[:, None, :]).astype(jnp.bfloat16)
    s2 = (sa[:, :, None] * cb[:, None, :] + ca[:, :, None] * sb[:, None, :]).astype(jnp.bfloat16)
    c2 = c2.reshape(P_SIZE, slab_rows)
    s2 = s2.reshape(P_SIZE, slab_rows)
    partial = jnp.einsum(
        "lu,ruj->lrj", c2, transformed[:, :, :j_len], preferred_element_type=jnp.float32
    ) - jnp.einsum("lu,ruj->lrj", s2, transformed[:, :, j_len:], preferred_element_type=jnp.float32)
    chan_count = lax.axis_size("chan")
    partial = partial.reshape(chan_count, P_SIZE // chan_count, NF, j_len)
    partial = lax.all_to_all(partial.astype(jnp.bfloat16), "chan", split_axis=0, concat_axis=0, tiled=True)
    partial = jnp.sum(partial.astype(jnp.float32), axis=0)
    partial = partial.reshape(P_SIZE // chan_count, NF, tile_count, j_len // tile_count)
    partial = jnp.transpose(partial, (2, 0, 1, 3))
    partial = lax.all_to_all(partial.astype(jnp.bfloat16), "tile", split_axis=0, concat_axis=0, tiled=True)
    partial = jnp.sum(partial.astype(jnp.float32), axis=0)
    out = jnp.transpose(partial, (0, 2, 1))
    return out.reshape(out.shape[0], -1) * (1.0 / G)


def solution(mesh):
    placed = (
        P("chan", "tile", None),
        P("chan", None, None, None, None),
        P("chan", "tile", None),
        P("chan", "tile"),
        P("chan", "tile"),
    )
    return jax.shard_map(
        local, mesh=mesh, in_specs=placed, out_specs=P("chan", "tile"), check_vma=False
    )
```

```python
import math

import jax
import jax.numpy as jnp
from jax import lax
from jax.sharding import PartitionSpec as P
from jax.experimental import pallas as pl
from jax.experimental.pallas import tpu as pltpu

G = 8192
S = 64
NW = 32
P_SIZE = 1024
NF = 8


def block_patches(samples, kernel_rows):
    sample_count = samples.shape[1] // 2
    support = kernel_rows.shape[3] // 2
    vis_real = samples[:, :sample_count, None]
    vis_imag = samples[:, sample_count:, None]
    kern_real = kernel_rows[:, 0].astype(jnp.float32)
    kern_imag = kernel_rows[:, 1].astype(jnp.float32)
    full_real = (vis_real * kern_real - vis_imag * kern_imag).astype(jnp.bfloat16)
    full_imag = (vis_real * kern_imag + vis_imag * kern_real).astype(jnp.bfloat16)
    weighted_real = full_real[:, :, support:]
    weighted_imag = full_imag[:, :, support:]
    v_weighted = jnp.stack(
        [
            jnp.concatenate([weighted_real, weighted_imag], axis=-1),
            jnp.concatenate([-weighted_imag, weighted_real], axis=-1),
        ],
        1,
    )
    patch = jnp.einsum("bpkx,bpkn->bxn", kernel_rows, v_weighted, preferred_element_type=jnp.float32)
    return patch[:, :support, :]


PATCH_CHUNK = 128


def patch_kernel(plane_ref, samples_ref, u_ref, v_ref, out_ref):
    base = pl.program_id(0) * PATCH_CHUNK
    for j in range(PATCH_CHUNK):
        w = plane_ref[base + j]
        column = samples_ref[:, j : j + 1]
        vis_real = column[:S]
        vis_imag = column[S:]
        first = v_ref[w, 0].astype(jnp.float32)
        second = v_ref[w, 1].astype(jnp.float32)
        top = (vis_real * first + vis_imag * second).astype(jnp.bfloat16)
        bottom = (vis_real * second - vis_imag * first).astype(jnp.bfloat16)
        rhs = jnp.concatenate(
            [jnp.concatenate([top, bottom], axis=1), jnp.concatenate([bottom, -top], axis=1)], axis=0
        )
        both = lax.dot_general(u_ref[w], rhs, (((0,), (0,)), ((), ())), preferred_element_type=jnp.float32)
        out_ref[j, 0] = both[:S, : 2 * S].astype(jnp.bfloat16)
        out_ref[j, 1] = both[:S, 2 * S :].astype(jnp.bfloat16)


def patches_rotated(samples, planes, kernel_set):
    slots = samples.shape[0]
    u_kernel = kernel_set.reshape(NW, 2 * S, 2 * S)
    v_real = kernel_set[:, 0, :, S:]
    v_imag = kernel_set[:, 1, :, S:]
    v_parts = jnp.stack(
        [jnp.concatenate([v_real, v_imag], axis=-1), jnp.concatenate([-v_imag, v_real], axis=-1)], axis=1
    )
    grid_spec = pltpu.PrefetchScalarGridSpec(
        num_scalar_prefetch=1,
        grid=(slots // PATCH_CHUNK,),
        in_specs=[
            pl.BlockSpec((2 * S, PATCH_CHUNK), lambda i, p: (0, i)),
            pl.BlockSpec((NW, 2 * S, 2 * S), lambda i, p: (0, 0, 0)),
            pl.BlockSpec((NW, 2, S, 2 * S), lambda i, p: (0, 0, 0, 0)),
        ],
        out_specs=pl.BlockSpec((PATCH_CHUNK, 2, S, 2 * S), lambda i, p: (i, 0, 0, 0)),
    )
    return pl.pallas_call(
        patch_kernel,
        grid_spec=grid_spec,
        out_shape=jax.ShapeDtypeStruct((slots, 2, S, 2 * S), jnp.bfloat16),
        cost_estimate=pl.CostEstimate(
            flops=2 * slots * S * 2 * S * 4 * S, transcendentals=0, bytes_accessed=slots * 2 * S * 2 * S * 2 * 2
        ),
    )(planes, jnp.transpose(samples), u_kernel, v_parts)


def phase_index(rows, cols):
    spacing = G // P_SIZE - 1
    return jnp.mod(rows[:, None] * (spacing * cols[None, :]), G)


def cos_sin_f32(index):
    angle = index.astype(jnp.float32) * (2.0 * math.pi / G)
    return jnp.cos(angle), jnp.sin(angle)


def local(visibilities, kernels, destination, cell, plane):
    tile_count = lax.axis_size("tile")
    tile_index = lax.axis_index("tile")
    samples = visibilities[0]
    kernel_set = kernels[0]
    owners = destination[0, :, 0]
    blocks = samples.shape[0]
    capacity = 3 * blocks // tile_count
    spacing = G // P_SIZE - 1

    tiles = jnp.arange(tile_count, dtype=jnp.int32)
    onehot = (owners[:, None] == tiles[None, :]).astype(jnp.int32)
    rank = jnp.sum(jnp.cumsum(onehot, axis=0) * onehot, axis=1) - 1
    slot = jnp.arange(capacity, dtype=jnp.int32)
    pick = (owners[None, None, :] == tiles[:, None, None]) & (rank[None, None, :] == slot[None, :, None])
    pick = pick.astype(jnp.float32).reshape(tile_count * capacity, blocks)
    packed_meta = (cell[0] * NW + plane[0]).astype(jnp.float32)
    routed = jnp.dot(
        pick, jnp.concatenate([samples, packed_meta[:, None]], axis=1), precision=lax.Precision.HIGHEST
    )
    send_samples = routed[:, : samples.shape[1]].reshape(tile_count, capacity, samples.shape[1])
    send_meta = routed[:, samples.shape[1]].reshape(tile_count, capacity)
    meta_row = jnp.pad(send_meta, ((0, 0), (0, samples.shape[1] - capacity)))[:, None, :]
    arrived = lax.all_to_all(
        jnp.concatenate([send_samples, meta_row], axis=1), "tile", split_axis=0, concat_axis=0, tiled=True
    )
    slot_total = tile_count * capacity
    arrived_meta = arrived[:, capacity, :capacity].astype(jnp.int32).reshape(slot_total)
    arrived = arrived[:, :capacity, :].reshape(slot_total, samples.shape[1])

    slab_rows = G // tile_count
    row_cells = slab_rows // S
    cell_cols = G // S
    q_len = G // NF
    q_cells = q_len // S
    j_len = P_SIZE // NF

    cell_r = arrived_meta // NW
    plane_r = arrived_meta % NW
    p2 = patches_rotated(arrived, plane_r, kernel_set).reshape(slot_total * 2, S * 2 * S)

    a_s = cell_r // cell_cols
    cc_s = cell_r % cell_cols
    p_s = cc_s // q_cells
    qc_s = cc_s % q_cells
    resid = jnp.arange(NF, dtype=jnp.int32)
    a_c = jnp.repeat(a_s, 2)[None, :]
    qc_c = jnp.repeat(qc_s, 2)[None, :]
    p_c = jnp.repeat(p_s, 2)[None, :]
    k_c = (jnp.arange(slot_total * 2, dtype=jnp.int32) % 2)[None, :]
    ph_index = jnp.mod(spacing * (p_c - NF // 2) * resid[:, None], NF)
    half = math.sqrt(0.5)
    cos_v = jnp.where(
        ph_index == 0,
        1.0,
        jnp.where(
            ph_index == 4,
            -1.0,
            jnp.where((ph_index == 2) | (ph_index == 6), 0.0, jnp.where((ph_index == 1) | (ph_index == 7), half, -half)),
        ),
    )
    sin_v = jnp.where(
        (ph_index == 0) | (ph_index == 4),
        0.0,
        jnp.where(
            ph_index == 2,
            1.0,
            jnp.where(ph_index == 6, -1.0, jnp.where((ph_index == 1) | (ph_index == 3), half, -half)),
        ),
    )
    phase = jnp.where(k_c == 0, cos_v, sin_v)
    cell_id = jnp.arange(row_cells * q_cells, dtype=jnp.int32)[:, None]
    inside = (a_c == cell_id // q_cells) & (qc_c == cell_id % q_cells)
    l2 = jnp.where(inside[None, :, :], phase[:, None, :], 0.0).astype(jnp.bfloat16)
    l2 = l2.reshape(NF * row_cells * q_cells, slot_total * 2)
    folded = jnp.dot(l2, p2, preferred_element_type=jnp.float32).astype(jnp.bfloat16)
    folded = folded.reshape(NF, row_cells, q_cells // 8, 8, S, 2 * S)

    coarse = jnp.arange(q_cells, dtype=jnp.int32) * S
    fine = jnp.arange(S, dtype=jnp.int32)
    n_full = jnp.arange(2 * j_len, dtype=jnp.int32) % j_len
    j_full = resid[:, None] + NF * (n_full[None, :] - j_len // 2)
    y_full = jnp.arange(2 * S, dtype=jnp.int32) % S
    ca, sa = cos_sin_f32(jnp.mod(coarse[None, :, None] * (spacing * j_full[:, None, :]), G))
    cb, sb = cos_sin_f32(jnp.mod(y_full[None, :, None] * (spacing * j_full[:, None, :]), G))
    ca, sa, cb, sb = lax.optimization_barrier((ca, sa, cb, sb))
    ca = ca[:, :, None, :]
    sa = sa[:, :, None, :]
    cb = cb[:, None, :, :]
    sb = sb[:, None, :, :]
    c1 = (ca * cb - sa * sb).astype(jnp.bfloat16)
    s1 = (sa * cb + ca * sb).astype(jnp.bfloat16)
    ri_in = lax.broadcasted_iota(jnp.int32, (1, 1, 2 * S, 2 * j_len), 2) // S
    ri_out = lax.broadcasted_iota(jnp.int32, (1, 1, 2 * S, 2 * j_len), 3) // j_len
    w1 = jnp.where(ri_in == ri_out, c1, jnp.where(ri_in == 0, s1, -s1))
    transformed = jnp.einsum("rahqxk,rhqkn->raxn", folded, w1.reshape(NF, q_cells // 8, 8, 2 * S, 2 * j_len), preferred_element_type=jnp.float32)
    transformed = transformed.astype(jnp.bfloat16).reshape(NF, slab_rows, 2 * j_len)

    l_index = jnp.arange(P_SIZE, dtype=jnp.int32) - P_SIZE // 2
    lane_blocks = slab_rows // 128
    block_base = (tile_index * slab_rows - G // 2) + jnp.arange(lane_blocks, dtype=jnp.int32) * 128
    ca, sa = cos_sin_f32(phase_index(l_index, block_base))
    cb, sb = cos_sin_f32(phase_index(l_index, jnp.arange(128, dtype=jnp.int32)))
    ca, sa, cb, sb = lax.optimization_barrier((ca, sa, cb, sb))
    c2 = (ca[:, :, None] * cb[:, None, :] - sa[:, :, None] * sb[:, None, :]).astype(jnp.bfloat16)
    s2 = (sa[:, :, None] * cb[:, None, :] + ca[:, :, None] * sb[:, None, :]).astype(jnp.bfloat16)
    c2 = c2.reshape(P_SIZE, slab_rows)
    s2 = s2.reshape(P_SIZE, slab_rows)
    partial = jnp.einsum(
        "lu,ruj->lrj", c2, transformed[:, :, :j_len], preferred_element_type=jnp.float32
    ) - jnp.einsum("lu,ruj->lrj", s2, transformed[:, :, j_len:], preferred_element_type=jnp.float32)
    chan_count = lax.axis_size("chan")
    partial = partial.reshape(chan_count, P_SIZE // chan_count, NF, j_len)
    partial = lax.all_to_all(partial.astype(jnp.bfloat16), "chan", split_axis=0, concat_axis=0, tiled=True)
    partial = jnp.sum(partial.astype(jnp.float32), axis=0)
    partial = partial.reshape(P_SIZE // chan_count, NF, tile_count, j_len // tile_count)
    partial = jnp.transpose(partial, (2, 0, 1, 3))
    partial = lax.all_to_all(partial.astype(jnp.bfloat16), "tile", split_axis=0, concat_axis=0, tiled=True)
    partial = jnp.sum(partial.astype(jnp.float32), axis=0)
    out = jnp.transpose(partial, (0, 2, 1))
    return out.reshape(out.shape[0], -1) * (1.0 / G)


def solution(mesh):
    placed = (
        P("chan", "tile", None),
        P("chan", None, None, None, None),
        P("chan", "tile", None),
        P("chan", "tile"),
        P("chan", "tile"),
    )
    return jax.shard_map(
        local, mesh=mesh, in_specs=placed, out_specs=P("chan", "tile"), check_vma=False
    )
```
